128 devices in a mesh: row: 8 (over x, core), col: 16 (over y, z).
Axes of the slice: x: 4, y: 4, z: 4, core: 2. Of those that a mesh axis runs over, the one named last changes fastest.
Arguments:
- trajectory_activations: bfloat16 [1280, 5120], P('row', 'col'), may hold values from -6 to 6
- kept_clusters_mask: int32 [32], replicated, may hold values from 0 to 1, as said below
- piece_receiving_entry: int32 [160], replicated, may hold values from 0 to 7, as said below
- piece_opening_position: int32 [160], replicated, may hold values from 0 to 72, as said below
- switching_coefficients: bfloat16 [27648, 5120], P('row', 'col'), may hold values from -0.078125 to 0.078125
- expansion_coefficients: bfloat16 [27648, 5120], P('row', 'col'), may hold values from -0.078125 to 0.078125
- contraction_coefficients: bfloat16 [27648, 5120], P('row', 'col'), may hold values from -0.0390625 to 0.0390625
- adjoint_vector: bfloat16 [640, 5120], P('row', 'col'), may hold values from -1.5 to 1.5
Outputs:
- mixed: bfloat16 [640, 5120], P('row', 'col')
- grad_input: bfloat16 [640, 5120], P('row', 'col')
- grad_w_gate: float32 [27648, 5120], P('row', 'col')
- grad_w_up: float32 [27648, 5120], P('row', 'col')
- grad_w_down: float32 [27648, 5120], P('row', 'col')
The draws below stay inside these ranges and needn't reach their ends.
Inputs may be any that keep to these rules, and one draw needn't show every extreme that they name: `kept_clusters_mask`: exactly 16 groups are kept, among them all 4 groups of one row index of the rollout. `piece_receiving_entry`: only entries of kept groups' blocks matter. Each row index of the packed batch receives the blocks of exactly 2 kept groups. The kept blocks of one row index of the rollout send at most 5 blocks to one row index of the packed batch, and in every draw some send exactly 5. `piece_opening_position`: only entries of kept groups' blocks matter. Each is a multiple of 8; the kept blocks cover every row index's 80 packed tokens exactly once.
All inputs are finite; a program needn't handle non-finite values.
Results may differ from the reference program's by a relative error of at most 0.004.
Values may be sent and summed in bfloat16 or wider, within the bound.
No kernel may reach another device: no remote copies, remote signals or barrier semaphores. Data moves between devices by JAX's collectives and lax.ppermute only.
A program may use at most 192 MiB of HBM per device.

```python
import jax
import jax.numpy as jnp

D = 5120
FF = 27648
TOK_ROW = 80
BLOCK = 8
GRP_ROW = 4
CLUSTER_PIECES = 5
TOKENS = 640
ROLL = 1280
GROUPS = 32
KEEP = 16
BLOCKS = 160


def packing_plan(key):
    base = jax.random.fold_in(key, 4242)
    keys = jax.random.split(base, 6)
    n_rows = TOKENS // TOK_ROW
    slots = TOK_ROW // BLOCK
    owner = jnp.arange(GROUPS, dtype=jnp.int32) // GRP_ROW
    busiest = jax.random.randint(keys[0], (), 0, n_rows, dtype=jnp.int32)
    priority = jax.random.permutation(keys[1], GROUPS).astype(jnp.int32)
    priority = jnp.where(owner == busiest, priority - GROUPS, priority)
    ranking = jnp.sum((priority[None, :] < priority[:, None]).astype(jnp.int32), axis=1)
    kept = (ranking < KEEP).astype(jnp.int32)
    position = jnp.cumsum(kept) - 1
    dest_perm = jax.random.permutation(keys[2], n_rows).astype(jnp.int32)
    group_dest = dest_perm[jnp.remainder(position, n_rows)]
    group_half = position // n_rows
    slot_table = jax.random.permutation(keys[3], jnp.tile(jnp.arange(slots, dtype=jnp.int32)[None, :], (n_rows, 1)), axis=1, independent=True)
    block_group = jnp.arange(BLOCKS, dtype=jnp.int32) // CLUSTER_PIECES
    block_part = jnp.arange(BLOCKS, dtype=jnp.int32) % CLUSTER_PIECES
    survival_indicator = kept[block_group]
    dest_live = group_dest[block_group]
    slot_index = jnp.clip(group_half[block_group] * CLUSTER_PIECES + block_part, 0, slots - 1)
    offset_live = BLOCK * slot_table[dest_live, slot_index]
    dest_other = jax.random.randint(keys[4], (BLOCKS,), 0, n_rows, dtype=jnp.int32)
    offset_other = BLOCK * jax.random.randint(keys[5], (BLOCKS,), 0, slots, dtype=jnp.int32)
    dest_final = jnp.where(survival_indicator == 1, dest_live, dest_other).astype(jnp.int32)
    offset_final = jnp.where(survival_indicator == 1, offset_live, offset_other).astype(jnp.int32)
    return (kept, dest_final, offset_final)


def draw_kept_clusters_mask(key, part):
    return packing_plan(key)[0]


def draw_piece_receiving_entry(key, part):
    return packing_plan(key)[1]


def draw_piece_opening_position(key, part):
    return packing_plan(key)[2]


def level_of(stream_key, shape, pieces, smallest, high):
    gain, own = 1.0, jax.random.fold_in(stream_key, 6)
    for axis_at, blocks in pieces:
        draws = jnp.exp(jax.random.uniform(jax.random.fold_in(own, axis_at), (blocks,), jnp.float32, smallest / len(pieces), high / len(pieces)))
        gain = gain * jnp.repeat(draws, shape[axis_at] // blocks).reshape([-1 if axis == axis_at else 1 for axis in range(len(shape))])
    return gain


def scatter_about(own_key, dims, scale, limit, cuts=(), kind=jnp.bfloat16):
    values = jax.random.normal(own_key, dims, jnp.float32) * scale
    if len(cuts) > 0:
        values = level_of(own_key, dims, cuts, -0.22, 0.18) * values
    return jnp.clip(values, min=-limit, max=limit).astype(kind)


def setup_inputs(seed: int = 0) -> dict:
    seeds = jax.random.split(jax.random.key(seed), 9)
    trajectory_activations = scatter_about(seeds[0], (ROLL, D), 1.0, 6.0, ((0, 8), (1, 16)))
    kept_clusters_mask = draw_kept_clusters_mask(jax.random.fold_in(seeds[8], 71), 0)
    piece_receiving_entry = draw_piece_receiving_entry(jax.random.fold_in(seeds[8], 71), 0)
    piece_opening_position = draw_piece_opening_position(jax.random.fold_in(seeds[8], 71), 0)
    switching_coefficients = scatter_about(seeds[4], (FF, D), D ** -0.5, 0.078125, ((0, 8), (1, 16)))
    expansion_coefficients = scatter_about(seeds[5], (FF, D), D ** -0.5, 0.078125, ((0, 8), (1, 16)))
    contraction_coefficients = scatter_about(seeds[6], (FF, D), FF ** -0.5, 0.0390625, ((0, 8), (1, 16)))
    adjoint_vector = scatter_about(seeds[7], (TOKENS, D), 0.25, 1.5, ((0, 8), (1, 16)))
    return {"trajectory_activations": trajectory_activations, "kept_clusters_mask": kept_clusters_mask, "piece_receiving_entry": piece_receiving_entry, "piece_opening_position": piece_opening_position, "switching_coefficients": switching_coefficients, "expansion_coefficients": expansion_coefficients, "contraction_coefficients": contraction_coefficients, "adjoint_vector": adjoint_vector}


def dense_emitters(kept_clusters_mask, piece_receiving_entry, piece_opening_position):
    blocks = piece_receiving_entry.shape[0]
    cluster_mapping = jnp.arange(blocks, dtype=jnp.int32) // CLUSTER_PIECES
    survival_indicator = kept_clusters_mask[cluster_mapping] == 1
    first_token = (piece_receiving_entry * TOK_ROW + piece_opening_position).astype(jnp.int32)
    within = jnp.arange(BLOCK, dtype=jnp.int32)
    target = jnp.where(survival_indicator[:, None], first_token[:, None] + within[None, :], TOKENS)
    target = target.reshape(-1).astype(jnp.int32)
    source = jnp.arange(blocks * BLOCK, dtype=jnp.int32)
    return jnp.zeros((TOKENS,), jnp.int32).at[target].set(source, mode="drop")


def reference(trajectory_activations, kept_clusters_mask, piece_receiving_entry, piece_opening_position, switching_coefficients, expansion_coefficients, contraction_coefficients, adjoint_vector):
    emitter_sequence = dense_emitters(kept_clusters_mask, piece_receiving_entry, piece_opening_position)
    packed = jnp.take(trajectory_activations, emitter_sequence, axis=0)
    gate_proj = jnp.dot(packed, switching_coefficients.T, preferred_element_type=jnp.float32)
    up_proj = jnp.dot(packed, expansion_coefficients.T, preferred_element_type=jnp.float32)
    sig_gate = jax.nn.sigmoid(gate_proj)
    hidden = (gate_proj * sig_gate * up_proj).astype(jnp.bfloat16)
    mixed = (packed.astype(jnp.float32) + jnp.dot(hidden, contraction_coefficients, preferred_element_type=jnp.float32)).astype(jnp.bfloat16)
    grad_hidden = jnp.dot(adjoint_vector, contraction_coefficients.T, preferred_element_type=jnp.float32)
    grad_gate = (grad_hidden * up_proj * sig_gate * (1.0 + gate_proj * (1.0 - sig_gate))).astype(jnp.bfloat16)
    grad_up = (grad_hidden * gate_proj * sig_gate).astype(jnp.bfloat16)
    grad_w_down = jnp.dot(hidden.T, adjoint_vector, preferred_element_type=jnp.float32)
    grad_w_gate = jnp.dot(grad_gate.T, packed, preferred_element_type=jnp.float32)
    grad_w_up = jnp.dot(grad_up.T, packed, preferred_element_type=jnp.float32)
    back_sum = jnp.dot(grad_gate, switching_coefficients, preferred_element_type=jnp.float32) + jnp.dot(grad_up, expansion_coefficients, preferred_element_type=jnp.float32)
    grad_input = (adjoint_vector.astype(jnp.float32) + back_sum).astype(jnp.bfloat16)
    return mixed, grad_input, grad_w_gate, grad_w_up, grad_w_down
```

```python
import jax
import jax.numpy as jnp
from jax import lax
from jax.sharding import Mesh
from jax.sharding import PartitionSpec as P

TOK_ROW = 80
BLOCK = 8
CLUSTER_PIECES = 5
CZ = 4


def piece_recipients(kept_clusters_mask, piece_receiving_entry):
    cluster_sequence = kept_clusters_mask.shape[0]
    survival_indicator = jnp.broadcast_to(
        kept_clusters_mask[:, None] == 1, (cluster_sequence, CLUSTER_PIECES)
    ).reshape(-1)
    return jnp.where(survival_indicator, piece_receiving_entry, -1)


def slot_ranking(live_dest):
    per_source = live_dest.shape[1]
    same_dest = (live_dest[:, :, None] == live_dest[:, None, :]) & (live_dest[:, None, :] >= 0)
    positions = jnp.arange(per_source, dtype=jnp.int32)
    earlier = positions[None, :] < positions[:, None]
    return jnp.sum((same_dest & earlier[None, :, :]).astype(jnp.int32), axis=2)


def pack_rows(trajectory_activations, kept_clusters_mask, piece_receiving_entry, piece_opening_position):
    row_count = lax.axis_size("row")
    row_here = lax.axis_index("row")
    feature_cols = trajectory_activations.shape[1]
    within = jnp.arange(BLOCK, dtype=jnp.int32)
    receiving_entries_total = piece_recipients(kept_clusters_mask, piece_receiving_entry)
    per_source = receiving_entries_total.shape[0] // row_count
    live_dest = receiving_entries_total.reshape(row_count, per_source)
    slot_rank = slot_ranking(live_dest)
    capacity = CLUSTER_PIECES * BLOCK
    my_dest = lax.dynamic_index_in_dim(live_dest, row_here, 0, keepdims=False)
    my_rank = lax.dynamic_index_in_dim(slot_rank, row_here, 0, keepdims=False)
    bucket_row = my_dest * capacity + my_rank * BLOCK
    bucket_row = jnp.where(
        my_dest[:, None] >= 0, bucket_row[:, None] + within[None, :], -1
    ).reshape(-1)
    selector = (
        jnp.arange(row_count * capacity, dtype=jnp.int32)[:, None] == bucket_row[None, :]
    ).astype(jnp.bfloat16)
    bucket = jnp.dot(selector, trajectory_activations, preferred_element_type=jnp.float32).astype(
        jnp.bfloat16
    )
    arrived = lax.all_to_all(
        bucket.reshape(row_count, capacity, feature_cols),
        "row",
        split_axis=0,
        concat_axis=0,
        tiled=True,
    )
    offsets = piece_opening_position.reshape(row_count, per_source)
    slot_ids = jnp.arange(CLUSTER_PIECES, dtype=jnp.int32)
    matched = (live_dest[:, None, :] == row_here) & (
        slot_rank[:, None, :] == slot_ids[None, :, None]
    )
    present = jnp.any(matched, axis=2)
    first_token = jnp.sum(jnp.where(matched, offsets[:, None, :], 0), axis=2)
    token_of = jnp.where(
        present[:, :, None], first_token[:, :, None] + within[None, None, :], -1
    ).reshape(-1)
    placing = (jnp.arange(TOK_ROW, dtype=jnp.int32)[:, None] == token_of[None, :]).astype(
        jnp.bfloat16
    )
    flat_arrived = arrived.reshape(row_count * capacity, feature_cols)
    return jnp.dot(placing, flat_arrived, preferred_element_type=jnp.float32).astype(jnp.bfloat16)


def per_device(
    trajectory_activations,
    kept_clusters_mask,
    piece_receiving_entry,
    piece_opening_position,
    switching_coefficients,
    expansion_coefficients,
    contraction_coefficients,
    adjoint_vector,
):
    row_count = lax.axis_size("row")
    cy_count = lax.axis_size("cy")
    cz_count = lax.axis_size("cz")
    col_count = cy_count * cz_count
    cz_here = lax.axis_index("cz")
    units, width = switching_coefficients.shape
    chunk = units // col_count
    tok_local = adjoint_vector.shape[0]
    tokens = tok_local * row_count

    w3 = jnp.stack((switching_coefficients, expansion_coefficients, contraction_coefficients))
    w3 = w3.reshape(3, cy_count, cz_count, chunk, width)
    w3 = lax.all_to_all(w3, "cz", split_axis=2, concat_axis=2, tiled=True)
    w_blk = jnp.transpose(w3, (0, 1, 3, 2, 4)).reshape(3, cy_count * chunk, cz_count * width)

    local_rows = pack_rows(
        trajectory_activations, kept_clusters_mask, piece_receiving_entry, piece_opening_position
    )
    xc = jnp.stack((local_rows, adjoint_vector))[None]
    xc_all = lax.all_gather(xc, ("row", "cz"), axis=0, tiled=True)
    xc_all = xc_all.reshape(row_count, cz_count, 2, tok_local, width)
    xc_blk = jnp.transpose(xc_all, (2, 0, 3, 1, 4)).reshape(2, tokens, cz_count * width)
    xc_own = lax.dynamic_index_in_dim(xc_all, cz_here, 1, keepdims=False)
    xc_own = jnp.transpose(xc_own, (1, 0, 2, 3)).reshape(2, tokens, width)
    x_panel = xc_own[0]
    cot_panel = xc_own[1]

    dn = (((1,), (1,)), ((), ()))
    gu = lax.dot_general(
        w_blk[:2].reshape(2 * cy_count * chunk, cz_count * width), xc_blk[0], dn,
        preferred_element_type=jnp.float32,
    )
    gh = lax.dot_general(w_blk[2], xc_blk[1], dn, preferred_element_type=jnp.float32)
    parts = jnp.concatenate(
        (gu.reshape(2, cy_count, chunk, tokens), gh.reshape(1, cy_count, chunk, tokens)), axis=0
    )
    parts = jnp.transpose(parts, (1, 0, 2, 3))
    sums = lax.psum_scatter(parts, "cy", scatter_dimension=0, tiled=True)[0]
    gate_proj = sums[0]
    up_proj = sums[1]
    grad_hidden = sums[2]
    sig_gate = jax.nn.sigmoid(gate_proj)
    hidden = (gate_proj * sig_gate * up_proj).astype(jnp.bfloat16)
    grad_gate = (grad_hidden * up_proj * sig_gate * (1.0 + gate_proj * (1.0 - sig_gate))).astype(
        jnp.bfloat16
    )
    grad_up = (grad_hidden * gate_proj * sig_gate).astype(jnp.bfloat16)
    acts = jnp.stack((hidden, grad_gate, grad_up))[None]
    acts_all = lax.all_gather(acts, ("cy", "cz"), axis=0, tiled=True)

    wg3 = switching_coefficients.reshape(col_count, chunk, width)
    wu3 = expansion_coefficients.reshape(col_count, chunk, width)
    wd3 = contraction_coefficients.reshape(col_count, chunk, width)
    h_all = acts_all[:, 0]
    gg_all = acts_all[:, 1]
    gu_all = acts_all[:, 2]
    dn_f = (((0, 1), (0, 1)), ((), ()))
    mixed_part = lax.dot_general(h_all, wd3, dn_f, preferred_element_type=jnp.float32)
    input_part = lax.dot_general(
        gg_all, wg3, dn_f, preferred_element_type=jnp.float32
    ) + lax.dot_general(gu_all, wu3, dn_f, preferred_element_type=jnp.float32)
    dn_t = (((2,), (0,)), ((), ()))
    grad_w_down = lax.dot_general(h_all, cot_panel, dn_t, preferred_element_type=jnp.float32)
    grad_w_gate = lax.dot_general(gg_all, x_panel, dn_t, preferred_element_type=jnp.float32)
    grad_w_up = lax.dot_general(gu_all, x_panel, dn_t, preferred_element_type=jnp.float32)

    both = jnp.concatenate((mixed_part, input_part), axis=1)
    both = lax.psum_scatter(both, "row", scatter_dimension=0, tiled=True)
    mixed = (local_rows.astype(jnp.float32) + both[:, :width]).astype(jnp.bfloat16)
    grad_input = (adjoint_vector.astype(jnp.float32) + both[:, width:]).astype(jnp.bfloat16)
    return (
        mixed,
        grad_input,
        grad_w_gate.reshape(units, width),
        grad_w_up.reshape(units, width),
        grad_w_down.reshape(units, width),
    )


def solution(mesh):
    rows, cols = mesh.devices.shape
    mesh3 = Mesh(mesh.devices.reshape(rows, cols // CZ, CZ), ("row", "cy", "cz"))
    blk = P("row", ("cy", "cz"))
    return jax.shard_map(
        per_device,
        mesh=mesh3,
        in_specs=(blk, P(), P(), P(), blk, blk, blk, blk),
        out_specs=(blk, blk, blk, blk, blk),
        check_vma=False,
    )
```

```python
import jax
import jax.numpy as jnp
from jax import lax
from jax.sharding import Mesh
from jax.sharding import PartitionSpec as P

TOK_ROW = 80
BLOCK = 8
CLUSTER_PIECES = 5
CZ = 4


def piece_recipients(kept_clusters_mask, piece_receiving_entry):
    cluster_sequence = kept_clusters_mask.shape[0]
    survival_indicator = jnp.broadcast_to(
        kept_clusters_mask[:, None] == 1, (cluster_sequence, CLUSTER_PIECES)
    ).reshape(-1)
    return jnp.where(survival_indicator, piece_receiving_entry, -1)


def slot_ranking(live_dest):
    per_source = live_dest.shape[1]
    same_dest = (live_dest[:, :, None] == live_dest[:, None, :]) & (live_dest[:, None, :] >= 0)
    positions = jnp.arange(per_source, dtype=jnp.int32)
    earlier = positions[None, :] < positions[:, None]
    return jnp.sum((same_dest & earlier[None, :, :]).astype(jnp.int32), axis=2)


def pack_rows(trajectory_activations, kept_clusters_mask, piece_receiving_entry, piece_opening_position):
    row_count = lax.axis_size("row")
    row_here = lax.axis_index("row")
    feature_cols = trajectory_activations.shape[1]
    within = jnp.arange(BLOCK, dtype=jnp.int32)
    receiving_entries_total = piece_recipients(kept_clusters_mask, piece_receiving_entry)
    per_source = receiving_entries_total.shape[0] // row_count
    live_dest = receiving_entries_total.reshape(row_count, per_source)
    slot_rank = slot_ranking(live_dest)
    capacity = CLUSTER_PIECES * BLOCK
    my_dest = lax.dynamic_index_in_dim(live_dest, row_here, 0, keepdims=False)
    my_rank = lax.dynamic_index_in_dim(slot_rank, row_here, 0, keepdims=False)
    bucket_row = my_dest * capacity + my_rank * BLOCK
    bucket_row = jnp.where(
        my_dest[:, None] >= 0, bucket_row[:, None] + within[None, :], -1
    ).reshape(-1)
    selector = (
        jnp.arange(row_count * capacity, dtype=jnp.int32)[:, None] == bucket_row[None, :]
    ).astype(jnp.bfloat16)
    bucket = jnp.dot(selector, trajectory_activations, preferred_element_type=jnp.float32).astype(
        jnp.bfloat16
    )
    arrived = lax.all_to_all(
        bucket.reshape(row_count, capacity, feature_cols),
        "row",
        split_axis=0,
        concat_axis=0,
        tiled=True,
    )
    offsets = piece_opening_position.reshape(row_count, per_source)
    slot_ids = jnp.arange(CLUSTER_PIECES, dtype=jnp.int32)
    matched = (live_dest[:, None, :] == row_here) & (
        slot_rank[:, None, :] == slot_ids[None, :, None]
    )
    present = jnp.any(matched, axis=2)
    first_token = jnp.sum(jnp.where(matched, offsets[:, None, :], 0), axis=2)
    token_of = jnp.where(
        present[:, :, None], first_token[:, :, None] + within[None, None, :], -1
    ).reshape(-1)
    placing = (jnp.arange(TOK_ROW, dtype=jnp.int32)[:, None] == token_of[None, :]).astype(
        jnp.bfloat16
    )
    flat_arrived = arrived.reshape(row_count * capacity, feature_cols)
    return jnp.dot(placing, flat_arrived, preferred_element_type=jnp.float32).astype(jnp.bfloat16)


def per_device(
    trajectory_activations,
    kept_clusters_mask,
    piece_receiving_entry,
    piece_opening_position,
    switching_coefficients,
    expansion_coefficients,
    contraction_coefficients,
    adjoint_vector,
):
    row_count = lax.axis_size("row")
    cy_count = lax.axis_size("cy")
    cz_count = lax.axis_size("cz")
    col_count = cy_count * cz_count
    cz_here = lax.axis_index("cz")
    units, width = switching_coefficients.shape
    chunk = units // col_count
    tok_local = adjoint_vector.shape[0]
    tokens = tok_local * row_count

    weights = (switching_coefficients, expansion_coefficients, contraction_coefficients)
    cw = [(i, (i + 1) % cz_count) for i in range(cz_count)]
    ccw = [(i, (i - 1) % cz_count) for i in range(cz_count)]

    def piece(w, shift):
        w4 = w.reshape(cy_count, cz_count, chunk, width)
        return lax.dynamic_index_in_dim(w4, (cz_here + shift) % cz_count, 1, keepdims=False)

    half_j = cy_count // 2
    far = [piece(w, 2) for w in weights]
    recv_cw = lax.ppermute([piece(w, 1) for w in weights] + [f[:half_j] for f in far], "cz", cw)
    recv_ccw = lax.ppermute([piece(w, 3) for w in weights] + [f[half_j:] for f in far], "cz", ccw)
    relay_cw = lax.ppermute(recv_cw[3:], "cz", cw)
    relay_ccw = lax.ppermute(recv_ccw[3:], "cz", ccw)
    by_source = [
        (0, [piece(w, 0) for w in weights]),
        (-1, recv_cw[:3]),
        (1, recv_ccw[:3]),
        (2, [jnp.concatenate((a, b), axis=0) for a, b in zip(relay_cw, relay_ccw)]),
    ]

    local_rows = pack_rows(
        trajectory_activations, kept_clusters_mask, piece_receiving_entry, piece_opening_position
    )
    xc = jnp.stack((local_rows, adjoint_vector))[None]
    xc_all = lax.all_gather(xc, ("row", "cz"), axis=0, tiled=True)
    xc_all = xc_all.reshape(row_count, cz_count, 2, tok_local, width)

    def xc_of(src):
        own = lax.dynamic_index_in_dim(xc_all, src % cz_count, 1, keepdims=False)
        return jnp.transpose(own, (1, 0, 2, 3)).reshape(2, tokens, width)

    dn = (((1,), (1,)), ((), ()))
    partial = [None, None, None]
    for offset, pieces in by_source:
        xc_src = xc_of(cz_here + offset)
        if offset == 0:
            x_panel = xc_src[0]
            cot_panel = xc_src[1]
        for m in range(3):
            term = lax.dot_general(
                pieces[m].reshape(cy_count * chunk, width), xc_src[0 if m < 2 else 1], dn,
                preferred_element_type=jnp.float32,
            )
            partial[m] = term if partial[m] is None else partial[m] + term
    parts = [p.reshape(cy_count, chunk, tokens) for p in partial]

    cy_here = lax.axis_index("cy")
    up_ring = [(i, (i + 1) % cy_count) for i in range(cy_count)]
    down_ring = [(i, (i - 1) % cy_count) for i in range(cy_count)]
    half_t = tokens // 2

    def own_chunk(idx, lo, hi):
        return [lax.dynamic_index_in_dim(p, idx % cy_count, 0, keepdims=False)[:, lo:hi] for p in parts]

    acc_up = own_chunk(cy_here - 1, 0, half_t)
    acc_down = own_chunk(cy_here + 1, half_t, tokens)
    for step in range(1, cy_count):
        got_up = lax.ppermute(acc_up, "cy", up_ring)
        got_down = lax.ppermute(acc_down, "cy", down_ring)
        mine_up = own_chunk(cy_here - step - 1, 0, half_t)
        mine_down = own_chunk(cy_here + step + 1, half_t, tokens)
        acc_up = [a + b for a, b in zip(got_up, mine_up)]
        acc_down = [a + b for a, b in zip(got_down, mine_down)]
    gate_proj, up_proj, grad_hidden = [
        jnp.concatenate((a, b), axis=1) for a, b in zip(acc_up, acc_down)
    ]
    sig_gate = jax.nn.sigmoid(gate_proj)
    hidden = (gate_proj * sig_gate * up_proj).astype(jnp.bfloat16)
    grad_gate = (grad_hidden * up_proj * sig_gate * (1.0 + gate_proj * (1.0 - sig_gate))).astype(
        jnp.bfloat16
    )
    grad_up = (grad_hidden * gate_proj * sig_gate).astype(jnp.bfloat16)
    acts = jnp.stack((hidden, grad_gate, grad_up))[None]
    acts_all = lax.all_gather(acts, ("cy", "cz"), axis=0, tiled=True)

    wg3 = switching_coefficients.reshape(col_count, chunk, width)
    wu3 = expansion_coefficients.reshape(col_count, chunk, width)
    wd3 = contraction_coefficients.reshape(col_count, chunk, width)
    h_all = acts_all[:, 0]
    gg_all = acts_all[:, 1]
    gu_all = acts_all[:, 2]
    dn_f = (((0, 1), (0, 1)), ((), ()))
    mixed_part = lax.dot_general(h_all, wd3, dn_f, preferred_element_type=jnp.float32)
    input_part = lax.dot_general(
        gg_all, wg3, dn_f, preferred_element_type=jnp.float32
    ) + lax.dot_general(gu_all, wu3, dn_f, preferred_element_type=jnp.float32)
    dn_t = (((2,), (0,)), ((), ()))
    grad_w_down = lax.dot_general(h_all, cot_panel, dn_t, preferred_element_type=jnp.float32)
    grad_w_gate = lax.dot_general(gg_all, x_panel, dn_t, preferred_element_type=jnp.float32)
    grad_w_up = lax.dot_general(gu_all, x_panel, dn_t, preferred_element_type=jnp.float32)

    both = jnp.concatenate((mixed_part, input_part), axis=1)
    both = lax.psum_scatter(both, "row", scatter_dimension=0, tiled=True)
    mixed = (local_rows.astype(jnp.float32) + both[:, :width]).astype(jnp.bfloat16)
    grad_input = (adjoint_vector.astype(jnp.float32) + both[:, width:]).astype(jnp.bfloat16)
    return (
        mixed,
        grad_input,
        grad_w_gate.reshape(units, width),
        grad_w_up.reshape(units, width),
        grad_w_down.reshape(units, width),
    )


def solution(mesh):
    rows, cols = mesh.devices.shape
    mesh3 = Mesh(mesh.devices.reshape(rows, cols // CZ, CZ), ("row", "cy", "cz"))
    blk = P("row", ("cy", "cz"))
    return jax.shard_map(
        per_device,
        mesh=mesh3,
        in_specs=(blk, P(), P(), P(), blk, blk, blk, blk),
        out_specs=(blk, blk, blk, blk, blk),
        check_vma=False,
    )
```

```python
import jax
import jax.numpy as jnp
from jax import lax
from jax.sharding import Mesh
from jax.sharding import PartitionSpec as P

TOK_ROW = 80
BLOCK = 8
CLUSTER_PIECES = 5
CZ = 4


def piece_recipients(kept_clusters_mask, piece_receiving_entry):
    cluster_sequence = kept_clusters_mask.shape[0]
    survival_indicator = jnp.broadcast_to(
        kept_clusters_mask[:, None] == 1, (cluster_sequence, CLUSTER_PIECES)
    ).reshape(-1)
    return jnp.where(survival_indicator, piece_receiving_entry, -1)


def slot_ranking(live_dest):
    per_source = live_dest.shape[1]
    same_dest = (live_dest[:, :, None] == live_dest[:, None, :]) & (live_dest[:, None, :] >= 0)
    positions = jnp.arange(per_source, dtype=jnp.int32)
    earlier = positions[None, :] < positions[:, None]
    return jnp.sum((same_dest & earlier[None, :, :]).astype(jnp.int32), axis=2)


def pack_rows(trajectory_activations, kept_clusters_mask, piece_receiving_entry, piece_opening_position):
    row_count = lax.axis_size("row")
    row_here = lax.axis_index("row")
    feature_cols = trajectory_activations.shape[1]
    within = jnp.arange(BLOCK, dtype=jnp.int32)
    receiving_entries_total = piece_recipients(kept_clusters_mask, piece_receiving_entry)
    per_source = receiving_entries_total.shape[0] // row_count
    live_dest = receiving_entries_total.reshape(row_count, per_source)
    slot_rank = slot_ranking(live_dest)
    capacity = CLUSTER_PIECES * BLOCK
    my_dest = lax.dynamic_index_in_dim(live_dest, row_here, 0, keepdims=False)
    my_rank = lax.dynamic_index_in_dim(slot_rank, row_here, 0, keepdims=False)
    bucket_row = my_dest * capacity + my_rank * BLOCK
    bucket_row = jnp.where(
        my_dest[:, None] >= 0, bucket_row[:, None] + within[None, :], -1
    ).reshape(-1)
    selector = (
        jnp.arange(row_count * capacity, dtype=jnp.int32)[:, None] == bucket_row[None, :]
    ).astype(jnp.bfloat16)
    bucket = jnp.dot(selector, trajectory_activations, preferred_element_type=jnp.float32).astype(
        jnp.bfloat16
    )
    arrived = lax.all_to_all(
        bucket.reshape(row_count, capacity, feature_cols),
        "row",
        split_axis=0,
        concat_axis=0,
        tiled=True,
    )
    offsets = piece_opening_position.reshape(row_count, per_source)
    slot_ids = jnp.arange(CLUSTER_PIECES, dtype=jnp.int32)
    matched = (live_dest[:, None, :] == row_here) & (
        slot_rank[:, None, :] == slot_ids[None, :, None]
    )
    present = jnp.any(matched, axis=2)
    first_token = jnp.sum(jnp.where(matched, offsets[:, None, :], 0), axis=2)
    token_of = jnp.where(
        present[:, :, None], first_token[:, :, None] + within[None, None, :], -1
    ).reshape(-1)
    placing = (jnp.arange(TOK_ROW, dtype=jnp.int32)[:, None] == token_of[None, :]).astype(
        jnp.bfloat16
    )
    flat_arrived = arrived.reshape(row_count * capacity, feature_cols)
    return jnp.dot(placing, flat_arrived, preferred_element_type=jnp.float32).astype(jnp.bfloat16)


def per_device(
    trajectory_activations,
    kept_clusters_mask,
    piece_receiving_entry,
    piece_opening_position,
    switching_coefficients,
    expansion_coefficients,
    contraction_coefficients,
    adjoint_vector,
):
    row_count = lax.axis_size("row")
    cy_count = lax.axis_size("cy")
    cz_count = lax.axis_size("cz")
    col_count = cy_count * cz_count
    cz_here = lax.axis_index("cz")
    units, width = switching_coefficients.shape
    chunk = units // col_count
    tok_local = adjoint_vector.shape[0]
    tokens = tok_local * row_count

    weights = (switching_coefficients, expansion_coefficients, contraction_coefficients)
    cw = [(i, (i + 1) % cz_count) for i in range(cz_count)]
    ccw = [(i, (i - 1) % cz_count) for i in range(cz_count)]

    span = cy_count * chunk

    def piece(w, shift):
        return lax.dynamic_slice_in_dim(w, ((cz_here + shift) % cz_count) * span, span, axis=0)

    half_j = span // 2
    far = [piece(w, 2) for w in weights]
    recv_cw = lax.ppermute([piece(w, 1) for w in weights] + [f[:half_j] for f in far], "cz", cw)
    recv_ccw = lax.ppermute([piece(w, 3) for w in weights] + [f[half_j:] for f in far], "cz", ccw)
    relay_cw = lax.ppermute(recv_cw[3:], "cz", cw)
    relay_ccw = lax.ppermute(recv_ccw[3:], "cz", ccw)
    by_source = [
        (0, [piece(w, 0) for w in weights]),
        (-1, recv_cw[:3]),
        (1, recv_ccw[:3]),
        (2, [jnp.concatenate((a, b), axis=0) for a, b in zip(relay_cw, relay_ccw)]),
    ]

    local_rows = pack_rows(
        trajectory_activations, kept_clusters_mask, piece_receiving_entry, piece_opening_position
    )
    xc = jnp.stack((local_rows, adjoint_vector))[None]
    xc_all = lax.all_gather(xc, ("row", "cz"), axis=0, tiled=True)
    xc_all = xc_all.reshape(row_count, cz_count, 2, tok_local, width)

    def xc_of(src):
        own = lax.dynamic_index_in_dim(xc_all, src % cz_count, 1, keepdims=False)
        return jnp.transpose(own, (1, 0, 2, 3)).reshape(2, tokens, width)

    dn = (((1,), (1,)), ((), ()))
    partial = [None, None, None]
    for offset, pieces in by_source:
        xc_src = xc_of(cz_here + offset)
        if offset == 0:
            x_panel = xc_src[0]
            cot_panel = xc_src[1]
        for m in range(3):
            term = lax.dot_general(
                pieces[m], xc_src[0 if m < 2 else 1], dn,
                preferred_element_type=jnp.float32,
            )
            partial[m] = term if partial[m] is None else partial[m] + term
    parts = [p.reshape(cy_count, chunk, tokens) for p in partial]

    cy_here = lax.axis_index("cy")
    up_ring = [(i, (i + 1) % cy_count) for i in range(cy_count)]
    down_ring = [(i, (i - 1) % cy_count) for i in range(cy_count)]
    half_t = tokens // 2

    def own_chunk(idx, lo, hi):
        return [lax.dynamic_index_in_dim(p, idx % cy_count, 0, keepdims=False)[:, lo:hi] for p in parts]

    acc_up = own_chunk(cy_here - 1, 0, half_t)
    acc_down = own_chunk(cy_here + 1, half_t, tokens)
    for step in range(1, cy_count):
        got_up = lax.ppermute(acc_up, "cy", up_ring)
        got_down = lax.ppermute(acc_down, "cy", down_ring)
        mine_up = own_chunk(cy_here - step - 1, 0, half_t)
        mine_down = own_chunk(cy_here + step + 1, half_t, tokens)
        acc_up = [a + b for a, b in zip(got_up, mine_up)]
        acc_down = [a + b for a, b in zip(got_down, mine_down)]
    gate_proj, up_proj, grad_hidden = [
        jnp.concatenate((a, b), axis=1) for a, b in zip(acc_up, acc_down)
    ]
    sig_gate = jax.nn.sigmoid(gate_proj)
    hidden = (gate_proj * sig_gate * up_proj).astype(jnp.bfloat16)
    grad_gate = (grad_hidden * up_proj * sig_gate * (1.0 + gate_proj * (1.0 - sig_gate))).astype(
        jnp.bfloat16
    )
    grad_up = (grad_hidden * gate_proj * sig_gate).astype(jnp.bfloat16)
    acts = jnp.stack((hidden, grad_gate, grad_up))[None]
    acts_all = lax.all_gather(acts, ("cz", "cy"), axis=0, tiled=True)
    h_all, gg_all, gu_all = [acts_all[:, m].reshape(units, tokens) for m in range(3)]
    dn_f = (((0,), (0,)), ((), ()))
    mixed_part = lax.dot_general(h_all, contraction_coefficients, dn_f, preferred_element_type=jnp.float32)
    input_part = lax.dot_general(
        gg_all, switching_coefficients, dn_f, preferred_element_type=jnp.float32
    ) + lax.dot_general(gu_all, expansion_coefficients, dn_f, preferred_element_type=jnp.float32)
    dn_t = (((1,), (0,)), ((), ()))
    grad_w_down = lax.dot_general(h_all, cot_panel, dn_t, preferred_element_type=jnp.float32)
    grad_w_gate = lax.dot_general(gg_all, x_panel, dn_t, preferred_element_type=jnp.float32)
    grad_w_up = lax.dot_general(gu_all, x_panel, dn_t, preferred_element_type=jnp.float32)

    both = jnp.concatenate((mixed_part, input_part), axis=1)
    both = lax.psum_scatter(both, "row", scatter_dimension=0, tiled=True)
    mixed = (local_rows.astype(jnp.float32) + both[:, :width]).astype(jnp.bfloat16)
    grad_input = (adjoint_vector.astype(jnp.float32) + both[:, width:]).astype(jnp.bfloat16)
    return (
        mixed,
        grad_input,
        grad_w_gate,
        grad_w_up,
        grad_w_down,
    )


def solution(mesh):
    rows, cols = mesh.devices.shape
    mesh3 = Mesh(mesh.devices.reshape(rows, cols // CZ, CZ), ("row", "cy", "cz"))
    blk = P("row", ("cy", "cz"))
    return jax.shard_map(
        per_device,
        mesh=mesh3,
        in_specs=(blk, P(), P(), P(), blk, blk, blk, blk),
        out_specs=(blk, blk, blk, blk, blk),
        check_vma=False,
    )
```

```python
import jax
import jax.numpy as jnp
from jax import lax
from jax.sharding import Mesh
from jax.sharding import PartitionSpec as P

TOK_ROW = 80
BLOCK = 8
CLUSTER_PIECES = 5
CZ = 4


def piece_recipients(kept_clusters_mask, piece_receiving_entry):
    cluster_sequence = kept_clusters_mask.shape[0]
    survival_indicator = jnp.broadcast_to(
        kept_clusters_mask[:, None] == 1, (cluster_sequence, CLUSTER_PIECES)
    ).reshape(-1)
    return jnp.where(survival_indicator, piece_receiving_entry, -1)


def slot_ranking(live_dest):
    per_source = live_dest.shape[1]
    same_dest = (live_dest[:, :, None] == live_dest[:, None, :]) & (live_dest[:, None, :] >= 0)
    positions = jnp.arange(per_source, dtype=jnp.int32)
    earlier = positions[None, :] < positions[:, None]
    return jnp.sum((same_dest & earlier[None, :, :]).astype(jnp.int32), axis=2)


def pack_rows(trajectory_activations, kept_clusters_mask, piece_receiving_entry, piece_opening_position):
    row_count = lax.axis_size("row")
    row_here = lax.axis_index("row")
    feature_cols = trajectory_activations.shape[1]
    within = jnp.arange(BLOCK, dtype=jnp.int32)
    receiving_entries_total = piece_recipients(kept_clusters_mask, piece_receiving_entry)
    per_source = receiving_entries_total.shape[0] // row_count
    live_dest = receiving_entries_total.reshape(row_count, per_source)
    slot_rank = slot_ranking(live_dest)
    capacity = CLUSTER_PIECES * BLOCK
    my_dest = lax.dynamic_index_in_dim(live_dest, row_here, 0, keepdims=False)
    my_rank = lax.dynamic_index_in_dim(slot_rank, row_here, 0, keepdims=False)
    bucket_row = my_dest * capacity + my_rank * BLOCK
    bucket_row = jnp.where(
        my_dest[:, None] >= 0, bucket_row[:, None] + within[None, :], -1
    ).reshape(-1)
    selector = (
        jnp.arange(row_count * capacity, dtype=jnp.int32)[:, None] == bucket_row[None, :]
    ).astype(jnp.bfloat16)
    bucket = jnp.dot(selector, trajectory_activations, preferred_element_type=jnp.float32).astype(
        jnp.bfloat16
    )
    arrived = lax.all_to_all(
        bucket.reshape(row_count, capacity, feature_cols),
        "row",
        split_axis=0,
        concat_axis=0,
        tiled=True,
    )
    offsets = piece_opening_position.reshape(row_count, per_source)
    slot_ids = jnp.arange(CLUSTER_PIECES, dtype=jnp.int32)
    matched = (live_dest[:, None, :] == row_here) & (
        slot_rank[:, None, :] == slot_ids[None, :, None]
    )
    present = jnp.any(matched, axis=2)
    first_token = jnp.sum(jnp.where(matched, offsets[:, None, :], 0), axis=2)
    token_of = jnp.where(
        present[:, :, None], first_token[:, :, None] + within[None, None, :], -1
    ).reshape(-1)
    placing = (jnp.arange(TOK_ROW, dtype=jnp.int32)[:, None] == token_of[None, :]).astype(
        jnp.bfloat16
    )
    flat_arrived = arrived.reshape(row_count * capacity, feature_cols)
    return jnp.dot(placing, flat_arrived, preferred_element_type=jnp.float32).astype(jnp.bfloat16)


def per_device(
    trajectory_activations,
    kept_clusters_mask,
    piece_receiving_entry,
    piece_opening_position,
    switching_coefficients,
    expansion_coefficients,
    contraction_coefficients,
    adjoint_vector,
):
    row_count = lax.axis_size("row")
    cy_count = lax.axis_size("cy")
    cz_count = lax.axis_size("cz")
    col_count = cy_count * cz_count
    cz_here = lax.axis_index("cz")
    units, width = switching_coefficients.shape
    chunk = units // col_count
    tok_local = adjoint_vector.shape[0]
    tokens = tok_local * row_count

    weights = (switching_coefficients, expansion_coefficients, contraction_coefficients)
    cw = [(i, (i + 1) % cz_count) for i in range(cz_count)]
    ccw = [(i, (i - 1) % cz_count) for i in range(cz_count)]

    span = cy_count * chunk

    def piece(w, shift):
        return lax.dynamic_slice_in_dim(w, ((cz_here + shift) % cz_count) * span, span, axis=0)

    half_j = span // 2
    far = jnp.stack([piece(w, 2) for w in weights])
    near_cw, half_cw, near_ccw, half_ccw = lax.ppermute(
        (jnp.stack([piece(w, 1) for w in weights]), far[:, :half_j]), "cz", cw
    ) + lax.ppermute((jnp.stack([piece(w, 3) for w in weights]), far[:, half_j:]), "cz", ccw)
    relay_cw = lax.ppermute(half_cw, "cz", cw)
    relay_ccw = lax.ppermute(half_ccw, "cz", ccw)
    by_source = [
        (0, [piece(w, 0) for w in weights]),
        (-1, near_cw),
        (1, near_ccw),
        (2, jnp.concatenate((relay_cw, relay_ccw), axis=1)),
    ]

    local_rows = pack_rows(
        trajectory_activations, kept_clusters_mask, piece_receiving_entry, piece_opening_position
    )
    xc = jnp.stack((local_rows, adjoint_vector))[None]
    xc_all = lax.all_gather(xc, ("row", "cz"), axis=0, tiled=True)
    xc_all = xc_all.reshape(row_count, cz_count, 2, tok_local, width)

    def xc_of(src):
        own = lax.dynamic_index_in_dim(xc_all, src % cz_count, 1, keepdims=False)
        return jnp.transpose(own, (1, 0, 2, 3)).reshape(2, tokens, width)

    dn = (((1,), (1,)), ((), ()))
    partial = [None, None, None]
    for offset, pieces in by_source:
        xc_src = xc_of(cz_here + offset)
        if offset == 0:
            x_panel = xc_src[0]
            cot_panel = xc_src[1]
        for m in range(3):
            term = lax.dot_general(
                pieces[m], xc_src[0 if m < 2 else 1], dn,
                preferred_element_type=jnp.float32,
            )
            partial[m] = term if partial[m] is None else partial[m] + term
    parts = [p.reshape(cy_count, chunk, tokens) for p in partial]

    cy_here = lax.axis_index("cy")
    up_ring = [(i, (i + 1) % cy_count) for i in range(cy_count)]
    down_ring = [(i, (i - 1) % cy_count) for i in range(cy_count)]
    half_t = tokens // 2

    def own_chunk(idx, lo, hi):
        return jnp.stack(
            [lax.dynamic_index_in_dim(p, idx % cy_count, 0, keepdims=False)[:, lo:hi] for p in parts]
        )

    acc_up = own_chunk(cy_here - 1, 0, half_t)
    acc_down = own_chunk(cy_here + 1, half_t, tokens)
    for step in range(1, cy_count):
        got_up = lax.ppermute(acc_up, "cy", up_ring)
        got_down = lax.ppermute(acc_down, "cy", down_ring)
        acc_up = got_up + own_chunk(cy_here - step - 1, 0, half_t)
        acc_down = got_down + own_chunk(cy_here + step + 1, half_t, tokens)
    gate_proj, up_proj, grad_hidden = jnp.concatenate((acc_up, acc_down), axis=2)
    sig_gate = jax.nn.sigmoid(gate_proj)
    hidden = (gate_proj * sig_gate * up_proj).astype(jnp.bfloat16)
    grad_gate = (grad_hidden * up_proj * sig_gate * (1.0 + gate_proj * (1.0 - sig_gate))).astype(
        jnp.bfloat16
    )
    grad_up = (grad_hidden * gate_proj * sig_gate).astype(jnp.bfloat16)
    acts = jnp.stack((hidden, grad_gate, grad_up))[None]
    acts_all = lax.all_gather(acts, ("cz", "cy"), axis=0, tiled=True)
    h_all, gg_all, gu_all = [acts_all[:, m].reshape(units, tokens) for m in range(3)]
    dn_f = (((0,), (0,)), ((), ()))
    mixed_part = lax.dot_general(h_all, contraction_coefficients, dn_f, preferred_element_type=jnp.float32)
    input_part = lax.dot_general(
        gg_all, switching_coefficients, dn_f, preferred_element_type=jnp.float32
    ) + lax.dot_general(gu_all, expansion_coefficients, dn_f, preferred_element_type=jnp.float32)
    dn_t = (((1,), (0,)), ((), ()))
    grad_w_down = lax.dot_general(h_all, cot_panel, dn_t, preferred_element_type=jnp.float32)
    grad_w_gate = lax.dot_general(gg_all, x_panel, dn_t, preferred_element_type=jnp.float32)
    grad_w_up = lax.dot_general(gu_all, x_panel, dn_t, preferred_element_type=jnp.float32)

    both = jnp.concatenate((mixed_part, input_part), axis=1)
    both = lax.psum_scatter(both, "row", scatter_dimension=0, tiled=True)
    mixed = (local_rows.astype(jnp.float32) + both[:, :width]).astype(jnp.bfloat16)
    grad_input = (adjoint_vector.astype(jnp.float32) + both[:, width:]).astype(jnp.bfloat16)
    return (
        mixed,
        grad_input,
        grad_w_gate,
        grad_w_up,
        grad_w_down,
    )


def solution(mesh):
    rows, cols = mesh.devices.shape
    mesh3 = Mesh(mesh.devices.reshape(rows, cols // CZ, CZ), ("row", "cy", "cz"))
    blk = P("row", ("cy", "cz"))
    return jax.shard_map(
        per_device,
        mesh=mesh3,
        in_specs=(blk, P(), P(), P(), blk, blk, blk, blk),
        out_specs=(blk, blk, blk, blk, blk),
        check_vma=False,
    )
```

```python
import jax
import jax.numpy as jnp
from jax import lax
from jax.sharding import Mesh
from jax.sharding import PartitionSpec as P

TOK_ROW = 80
BLOCK = 8
CLUSTER_PIECES = 5
CZ = 4


def piece_recipients(kept_clusters_mask, piece_receiving_entry):
    cluster_sequence = kept_clusters_mask.shape[0]
    survival_indicator = jnp.broadcast_to(
        kept_clusters_mask[:, None] == 1, (cluster_sequence, CLUSTER_PIECES)
    ).reshape(-1)
    return jnp.where(survival_indicator, piece_receiving_entry, -1)


def slot_ranking(live_dest):
    per_source = live_dest.shape[1]
    same_dest = (live_dest[:, :, None] == live_dest[:, None, :]) & (live_dest[:, None, :] >= 0)
    positions = jnp.arange(per_source, dtype=jnp.int32)
    earlier = positions[None, :] < positions[:, None]
    return jnp.sum((same_dest & earlier[None, :, :]).astype(jnp.int32), axis=2)


def pack_rows(trajectory_activations, kept_clusters_mask, piece_receiving_entry, piece_opening_position):
    row_count = lax.axis_size("row")
    row_here = lax.axis_index("row")
    feature_cols = trajectory_activations.shape[1]
    within = jnp.arange(BLOCK, dtype=jnp.int32)
    receiving_entries_total = piece_recipients(kept_clusters_mask, piece_receiving_entry)
    per_source = receiving_entries_total.shape[0] // row_count
    live_dest = receiving_entries_total.reshape(row_count, per_source)
    slot_rank = slot_ranking(live_dest)
    capacity = CLUSTER_PIECES * BLOCK
    my_dest = lax.dynamic_index_in_dim(live_dest, row_here, 0, keepdims=False)
    my_rank = lax.dynamic_index_in_dim(slot_rank, row_here, 0, keepdims=False)
    bucket_row = my_dest * capacity + my_rank * BLOCK
    bucket_row = jnp.where(
        my_dest[:, None] >= 0, bucket_row[:, None] + within[None, :], -1
    ).reshape(-1)
    selector = (
        jnp.arange(row_count * capacity, dtype=jnp.int32)[:, None] == bucket_row[None, :]
    ).astype(jnp.bfloat16)
    bucket = jnp.dot(selector, trajectory_activations, preferred_element_type=jnp.float32).astype(
        jnp.bfloat16
    )
    arrived = lax.all_to_all(
        bucket.reshape(row_count, capacity, feature_cols),
        "row",
        split_axis=0,
        concat_axis=0,
        tiled=True,
    )
    offsets = piece_opening_position.reshape(row_count, per_source)
    slot_ids = jnp.arange(CLUSTER_PIECES, dtype=jnp.int32)
    matched = (live_dest[:, None, :] == row_here) & (
        slot_rank[:, None, :] == slot_ids[None, :, None]
    )
    present = jnp.any(matched, axis=2)
    first_token = jnp.sum(jnp.where(matched, offsets[:, None, :], 0), axis=2)
    token_of = jnp.where(
        present[:, :, None], first_token[:, :, None] + within[None, None, :], -1
    ).reshape(-1)
    placing = (jnp.arange(TOK_ROW, dtype=jnp.int32)[:, None] == token_of[None, :]).astype(
        jnp.bfloat16
    )
    flat_arrived = arrived.reshape(row_count * capacity, feature_cols)
    return jnp.dot(placing, flat_arrived, preferred_element_type=jnp.float32).astype(jnp.bfloat16)


def per_device(
    trajectory_activations,
    kept_clusters_mask,
    piece_receiving_entry,
    piece_opening_position,
    switching_coefficients,
    expansion_coefficients,
    contraction_coefficients,
    adjoint_vector,
):
    row_count = lax.axis_size("row")
    cy_count = lax.axis_size("cy")
    cz_count = lax.axis_size("cz")
    col_count = cy_count * cz_count
    cz_here = lax.axis_index("cz")
    units, width = switching_coefficients.shape
    chunk = units // col_count
    tok_local = adjoint_vector.shape[0]
    tokens = tok_local * row_count

    weights = (switching_coefficients, expansion_coefficients, contraction_coefficients)
    cw = [(i, (i + 1) % cz_count) for i in range(cz_count)]
    ccw = [(i, (i - 1) % cz_count) for i in range(cz_count)]

    span = cy_count * chunk

    def piece(w, shift):
        return lax.dynamic_slice_in_dim(w, ((cz_here + shift) % cz_count) * span, span, axis=0)

    half_j = span // 2
    far = [piece(w, 2) for w in weights]
    recv_cw = lax.ppermute([piece(w, 1) for w in weights] + [f[:half_j] for f in far], "cz", cw)
    recv_ccw = lax.ppermute([piece(w, 3) for w in weights] + [f[half_j:] for f in far], "cz", ccw)
    relay_cw = lax.ppermute(recv_cw[3:], "cz", cw)
    relay_ccw = lax.ppermute(recv_ccw[3:], "cz", ccw)
    by_source = [
        (0, [piece(w, 0) for w in weights]),
        (-1, recv_cw[:3]),
        (1, recv_ccw[:3]),
        (2, [jnp.concatenate((a, b), axis=0) for a, b in zip(relay_cw, relay_ccw)]),
    ]

    local_rows = pack_rows(
        trajectory_activations, kept_clusters_mask, piece_receiving_entry, piece_opening_position
    )
    xc = jnp.stack((local_rows, adjoint_vector))[None]
    xc_all = lax.all_gather(xc, ("row", "cz"), axis=0, tiled=True)
    xc_all = xc_all.reshape(row_count, cz_count, 2, tok_local, width)

    def xc_of(src):
        own = lax.dynamic_index_in_dim(xc_all, src % cz_count, 1, keepdims=False)
        return jnp.transpose(own, (1, 0, 2, 3)).reshape(2, tokens, width)

    dn = (((1,), (1,)), ((), ()))
    partial = [None, None, None]
    for offset, pieces in by_source:
        xc_src = xc_of(cz_here + offset)
        if offset == 0:
            x_panel = xc_src[0]
            cot_panel = xc_src[1]
        for m in range(3):
            term = lax.dot_general(
                pieces[m], xc_src[0 if m < 2 else 1], dn,
                preferred_element_type=jnp.float32,
            )
            partial[m] = term if partial[m] is None else partial[m] + term
    parts = [p.reshape(cy_count, chunk, tokens) for p in partial]

    cy_here = lax.axis_index("cy")
    up_ring = [(i, (i + 1) % cy_count) for i in range(cy_count)]
    down_ring = [(i, (i - 1) % cy_count) for i in range(cy_count)]
    half_t = tokens // 2

    def own_chunk(idx, lo, hi):
        return [lax.dynamic_index_in_dim(p, idx % cy_count, 0, keepdims=False)[:, lo:hi] for p in parts]

    acc_up = own_chunk(cy_here - 1, 0, half_t)
    acc_down = own_chunk(cy_here + 1, half_t, tokens)
    for step in range(1, cy_count):
        got_up = lax.ppermute(acc_up, "cy", up_ring)
        got_down = lax.ppermute(acc_down, "cy", down_ring)
        mine_up = own_chunk(cy_here - step - 1, 0, half_t)
        mine_down = own_chunk(cy_here + step + 1, half_t, tokens)
        acc_up = [a + b for a, b in zip(got_up, mine_up)]
        acc_down = [a + b for a, b in zip(got_down, mine_down)]
    gate_proj, up_proj, grad_hidden = [
        jnp.concatenate((a, b), axis=1) for a, b in zip(acc_up, acc_down)
    ]
    sig_gate = jax.nn.sigmoid(gate_proj)
    hidden = (gate_proj * sig_gate * up_proj).astype(jnp.bfloat16)
    grad_gate = (grad_hidden * up_proj * sig_gate * (1.0 + gate_proj * (1.0 - sig_gate))).astype(
        jnp.bfloat16
    )
    grad_up = (grad_hidden * gate_proj * sig_gate).astype(jnp.bfloat16)
    h_all, gg_all, gu_all = [
        lax.all_gather(a, ("cz", "cy"), axis=0, tiled=True) for a in (hidden, grad_gate, grad_up)
    ]
    dn_f = (((0,), (0,)), ((), ()))
    mixed_part = lax.dot_general(h_all, contraction_coefficients, dn_f, preferred_element_type=jnp.float32)
    input_part = lax.dot_general(
        gg_all, switching_coefficients, dn_f, preferred_element_type=jnp.float32
    ) + lax.dot_general(gu_all, expansion_coefficients, dn_f, preferred_element_type=jnp.float32)
    dn_t = (((1,), (0,)), ((), ()))
    grad_w_down = lax.dot_general(h_all, cot_panel, dn_t, preferred_element_type=jnp.float32)
    grad_w_gate = lax.dot_general(gg_all, x_panel, dn_t, preferred_element_type=jnp.float32)
    grad_w_up = lax.dot_general(gu_all, x_panel, dn_t, preferred_element_type=jnp.float32)

    both = jnp.concatenate((mixed_part, input_part), axis=1)
    both = lax.psum_scatter(both, "row", scatter_dimension=0, tiled=True)
    mixed = (local_rows.astype(jnp.float32) + both[:, :width]).astype(jnp.bfloat16)
    grad_input = (adjoint_vector.astype(jnp.float32) + both[:, width:]).astype(jnp.bfloat16)
    return (
        mixed,
        grad_input,
        grad_w_gate,
        grad_w_up,
        grad_w_down,
    )


def solution(mesh):
    rows, cols = mesh.devices.shape
    mesh3 = Mesh(mesh.devices.reshape(rows, cols // CZ, CZ), ("row", "cy", "cz"))
    blk = P("row", ("cy", "cz"))
    return jax.shard_map(
        per_device,
        mesh=mesh3,
        in_specs=(blk, P(), P(), P(), blk, blk, blk, blk),
        out_specs=(blk, blk, blk, blk, blk),
        check_vma=False,
    )
```

```python
import jax
import jax.numpy as jnp
from jax import lax
from jax.sharding import Mesh
from jax.sharding import PartitionSpec as P

TOK_ROW = 80
BLOCK = 8
CLUSTER_PIECES = 5
CZ = 4


def piece_recipients(kept_clusters_mask, piece_receiving_entry):
    cluster_sequence = kept_clusters_mask.shape[0]
    survival_indicator = jnp.broadcast_to(
        kept_clusters_mask[:, None] == 1, (cluster_sequence, CLUSTER_PIECES)
    ).reshape(-1)
    return jnp.where(survival_indicator, piece_receiving_entry, -1)


def slot_ranking(live_dest):
    per_source = live_dest.shape[1]
    same_dest = (live_dest[:, :, None] == live_dest[:, None, :]) & (live_dest[:, None, :] >= 0)
    positions = jnp.arange(per_source, dtype=jnp.int32)
    earlier = positions[None, :] < positions[:, None]
    return jnp.sum((same_dest & earlier[None, :, :]).astype(jnp.int32), axis=2)


def pack_rows(trajectory_activations, kept_clusters_mask, piece_receiving_entry, piece_opening_position):
    row_count = lax.axis_size("row")
    row_here = lax.axis_index("row")
    feature_cols = trajectory_activations.shape[1]
    within = jnp.arange(BLOCK, dtype=jnp.int32)
    receiving_entries_total = piece_recipients(kept_clusters_mask, piece_receiving_entry)
    per_source = receiving_entries_total.shape[0] // row_count
    live_dest = receiving_entries_total.reshape(row_count, per_source)
    slot_rank = slot_ranking(live_dest)
    capacity = CLUSTER_PIECES * BLOCK
    my_dest = lax.dynamic_index_in_dim(live_dest, row_here, 0, keepdims=False)
    my_rank = lax.dynamic_index_in_dim(slot_rank, row_here, 0, keepdims=False)
    bucket_row = my_dest * capacity + my_rank * BLOCK
    bucket_row = jnp.where(
        my_dest[:, None] >= 0, bucket_row[:, None] + within[None, :], -1
    ).reshape(-1)
    selector = (
        jnp.arange(row_count * capacity, dtype=jnp.int32)[:, None] == bucket_row[None, :]
    ).astype(jnp.bfloat16)
    bucket = jnp.dot(selector, trajectory_activations, preferred_element_type=jnp.float32).astype(
        jnp.bfloat16
    )
    arrived = lax.all_to_all(
        bucket.reshape(row_count, capacity, feature_cols),
        "row",
        split_axis=0,
        concat_axis=0,
        tiled=True,
    )
    offsets = piece_opening_position.reshape(row_count, per_source)
    slot_ids = jnp.arange(CLUSTER_PIECES, dtype=jnp.int32)
    matched = (live_dest[:, None, :] == row_here) & (
        slot_rank[:, None, :] == slot_ids[None, :, None]
    )
    present = jnp.any(matched, axis=2)
    first_token = jnp.sum(jnp.where(matched, offsets[:, None, :], 0), axis=2)
    token_of = jnp.where(
        present[:, :, None], first_token[:, :, None] + within[None, None, :], -1
    ).reshape(-1)
    placing = (jnp.arange(TOK_ROW, dtype=jnp.int32)[:, None] == token_of[None, :]).astype(
        jnp.bfloat16
    )
    flat_arrived = arrived.reshape(row_count * capacity, feature_cols)
    return jnp.dot(placing, flat_arrived, preferred_element_type=jnp.float32).astype(jnp.bfloat16)


def per_device(
    trajectory_activations,
    kept_clusters_mask,
    piece_receiving_entry,
    piece_opening_position,
    switching_coefficients,
    expansion_coefficients,
    contraction_coefficients,
    adjoint_vector,
):
    row_count = lax.axis_size("row")
    cy_count = lax.axis_size("cy")
    cz_count = lax.axis_size("cz")
    col_count = cy_count * cz_count
    cz_here = lax.axis_index("cz")
    units, width = switching_coefficients.shape
    chunk = units // col_count
    tok_local = adjoint_vector.shape[0]
    tokens = tok_local * row_count

    cw = [(i, (i + 1) % cz_count) for i in range(cz_count)]
    ccw = [(i, (i - 1) % cz_count) for i in range(cz_count)]
    span = cy_count * chunk
    half_j = span // 2

    def piece(w, shift):
        return lax.dynamic_slice_in_dim(w, ((cz_here + shift) % cz_count) * span, span, axis=0)

    def reblock(weights):
        far = [piece(w, 2) for w in weights]
        n = len(weights)
        recv_cw = lax.ppermute([piece(w, 1) for w in weights] + [f[:half_j] for f in far], "cz", cw)
        recv_ccw = lax.ppermute([piece(w, 3) for w in weights] + [f[half_j:] for f in far], "cz", ccw)
        relay_cw = lax.ppermute(recv_cw[n:], "cz", cw)
        relay_ccw = lax.ppermute(recv_ccw[n:], "cz", ccw)
        return [
            (0, [piece(w, 0) for w in weights]),
            (-1, recv_cw[:n]),
            (1, recv_ccw[:n]),
            (2, [jnp.concatenate((a, b), axis=0) for a, b in zip(relay_cw, relay_ccw)]),
        ]

    gu_sources = reblock((switching_coefficients, expansion_coefficients))

    local_rows = pack_rows(
        trajectory_activations, kept_clusters_mask, piece_receiving_entry, piece_opening_position
    )
    xc = jnp.stack((local_rows, adjoint_vector))[None]
    xc_all = lax.all_gather(xc, ("row", "cz"), axis=0, tiled=True)
    xc_all = xc_all.reshape(row_count, cz_count, 2, tok_local, width)

    def xc_of(src):
        own = lax.dynamic_index_in_dim(xc_all, src % cz_count, 1, keepdims=False)
        return jnp.transpose(own, (1, 0, 2, 3)).reshape(2, tokens, width)

    dn = (((1,), (1,)), ((), ()))

    def width_sum(sources, which):
        out = [None] * len(which)
        for offset, pieces in sources:
            xc_src = xc_of(cz_here + offset)
            for m, use in enumerate(which):
                term = lax.dot_general(
                    pieces[m], xc_src[use], dn, preferred_element_type=jnp.float32
                )
                out[m] = term if out[m] is None else out[m] + term
        return [p.reshape(cy_count, chunk, tokens) for p in out]

    own_xc = xc_of(cz_here)
    x_panel = own_xc[0]
    cot_panel = own_xc[1]
    gu_parts = width_sum(gu_sources, (0, 0))
    wd_held, gu_parts = lax.optimization_barrier((contraction_coefficients, gu_parts))
    d_sources = reblock((wd_held,))

    cy_here = lax.axis_index("cy")
    up_ring = [(i, (i + 1) % cy_count) for i in range(cy_count)]
    down_ring = [(i, (i - 1) % cy_count) for i in range(cy_count)]
    half_t = tokens // 2

    def ring_sum(parts):
        def own_chunk(idx, lo, hi):
            return [lax.dynamic_index_in_dim(p, idx % cy_count, 0, keepdims=False)[:, lo:hi] for p in parts]

        acc_up = own_chunk(cy_here - 1, 0, half_t)
        acc_down = own_chunk(cy_here + 1, half_t, tokens)
        for step in range(1, cy_count):
            got_up = lax.ppermute(acc_up, "cy", up_ring)
            got_down = lax.ppermute(acc_down, "cy", down_ring)
            mine_up = own_chunk(cy_here - step - 1, 0, half_t)
            mine_down = own_chunk(cy_here + step + 1, half_t, tokens)
            acc_up = [a + b for a, b in zip(got_up, mine_up)]
            acc_down = [a + b for a, b in zip(got_down, mine_down)]
        return [jnp.concatenate((a, b), axis=1) for a, b in zip(acc_up, acc_down)]

    gate_proj, up_proj = ring_sum(gu_parts)
    (grad_hidden,) = ring_sum(width_sum(d_sources, (1,)))
    sig_gate = jax.nn.sigmoid(gate_proj)
    hidden = (gate_proj * sig_gate * up_proj).astype(jnp.bfloat16)
    grad_gate = (grad_hidden * up_proj * sig_gate * (1.0 + gate_proj * (1.0 - sig_gate))).astype(
        jnp.bfloat16
    )
    grad_up = (grad_hidden * gate_proj * sig_gate).astype(jnp.bfloat16)
    acts = jnp.stack((hidden, grad_gate, grad_up))[None]
    acts_all = lax.all_gather(acts, ("cz", "cy"), axis=0, tiled=True)
    h_all, gg_all, gu_all = [acts_all[:, m].reshape(units, tokens) for m in range(3)]
    dn_f = (((0,), (0,)), ((), ()))
    mixed_part = lax.dot_general(h_all, contraction_coefficients, dn_f, preferred_element_type=jnp.float32)
    input_part = lax.dot_general(
        gg_all, switching_coefficients, dn_f, preferred_element_type=jnp.float32
    ) + lax.dot_general(gu_all, expansion_coefficients, dn_f, preferred_element_type=jnp.float32)
    dn_t = (((1,), (0,)), ((), ()))
    grad_w_down = lax.dot_general(h_all, cot_panel, dn_t, preferred_element_type=jnp.float32)
    grad_w_gate = lax.dot_general(gg_all, x_panel, dn_t, preferred_element_type=jnp.float32)
    grad_w_up = lax.dot_general(gu_all, x_panel, dn_t, preferred_element_type=jnp.float32)

    both = jnp.concatenate((mixed_part, input_part), axis=1)
    both = lax.psum_scatter(both, "row", scatter_dimension=0, tiled=True)
    mixed = (local_rows.astype(jnp.float32) + both[:, :width]).astype(jnp.bfloat16)
    grad_input = (adjoint_vector.astype(jnp.float32) + both[:, width:]).astype(jnp.bfloat16)
    return (
        mixed,
        grad_input,
        grad_w_gate,
        grad_w_up,
        grad_w_down,
    )


def solution(mesh):
    rows, cols = mesh.devices.shape
    mesh3 = Mesh(mesh.devices.reshape(rows, cols // CZ, CZ), ("row", "cy", "cz"))
    blk = P("row", ("cy", "cz"))
    return jax.shard_map(
        per_device,
        mesh=mesh3,
        in_specs=(blk, P(), P(), P(), blk, blk, blk, blk),
        out_specs=(blk, blk, blk, blk, blk),
        check_vma=False,
    )
```

```python
import jax
import jax.numpy as jnp
from jax import lax
from jax.sharding import Mesh
from jax.sharding import PartitionSpec as P

TOK_ROW = 80
BLOCK = 8
CLUSTER_PIECES = 5
CZ = 4


def piece_recipients(kept_clusters_mask, piece_receiving_entry):
    cluster_sequence = kept_clusters_mask.shape[0]
    survival_indicator = jnp.broadcast_to(
        kept_clusters_mask[:, None] == 1, (cluster_sequence, CLUSTER_PIECES)
    ).reshape(-1)
    return jnp.where(survival_indicator, piece_receiving_entry, -1)


def slot_ranking(live_dest):
    per_source = live_dest.shape[1]
    same_dest = (live_dest[:, :, None] == live_dest[:, None, :]) & (live_dest[:, None, :] >= 0)
    positions = jnp.arange(per_source, dtype=jnp.int32)
    earlier = positions[None, :] < positions[:, None]
    return jnp.sum((same_dest & earlier[None, :, :]).astype(jnp.int32), axis=2)


def pack_rows(trajectory_activations, kept_clusters_mask, piece_receiving_entry, piece_opening_position):
    row_count = lax.axis_size("row")
    row_here = lax.axis_index("row")
    feature_cols = trajectory_activations.shape[1]
    within = jnp.arange(BLOCK, dtype=jnp.int32)
    receiving_entries_total = piece_recipients(kept_clusters_mask, piece_receiving_entry)
    per_source = receiving_entries_total.shape[0] // row_count
    live_dest = receiving_entries_total.reshape(row_count, per_source)
    slot_rank = slot_ranking(live_dest)
    capacity = CLUSTER_PIECES * BLOCK
    my_dest = lax.dynamic_index_in_dim(live_dest, row_here, 0, keepdims=False)
    my_rank = lax.dynamic_index_in_dim(slot_rank, row_here, 0, keepdims=False)
    bucket_row = my_dest * capacity + my_rank * BLOCK
    bucket_row = jnp.where(
        my_dest[:, None] >= 0, bucket_row[:, None] + within[None, :], -1
    ).reshape(-1)
    selector = (
        jnp.arange(row_count * capacity, dtype=jnp.int32)[:, None] == bucket_row[None, :]
    ).astype(jnp.bfloat16)
    bucket = jnp.dot(selector, trajectory_activations, preferred_element_type=jnp.float32).astype(
        jnp.bfloat16
    )
    arrived = lax.all_to_all(
        bucket.reshape(row_count, capacity, feature_cols),
        "row",
        split_axis=0,
        concat_axis=0,
        tiled=True,
    )
    offsets = piece_opening_position.reshape(row_count, per_source)
    slot_ids = jnp.arange(CLUSTER_PIECES, dtype=jnp.int32)
    matched = (live_dest[:, None, :] == row_here) & (
        slot_rank[:, None, :] == slot_ids[None, :, None]
    )
    present = jnp.any(matched, axis=2)
    first_token = jnp.sum(jnp.where(matched, offsets[:, None, :], 0), axis=2)
    token_of = jnp.where(
        present[:, :, None], first_token[:, :, None] + within[None, None, :], -1
    ).reshape(-1)
    placing = (jnp.arange(TOK_ROW, dtype=jnp.int32)[:, None] == token_of[None, :]).astype(
        jnp.bfloat16
    )
    flat_arrived = arrived.reshape(row_count * capacity, feature_cols)
    return jnp.dot(placing, flat_arrived, preferred_element_type=jnp.float32).astype(jnp.bfloat16)


def per_device(
    trajectory_activations,
    kept_clusters_mask,
    piece_receiving_entry,
    piece_opening_position,
    switching_coefficients,
    expansion_coefficients,
    contraction_coefficients,
    adjoint_vector,
):
    row_count = lax.axis_size("row")
    cy_count = lax.axis_size("cy")
    cz_count = lax.axis_size("cz")
    col_count = cy_count * cz_count
    cz_here = lax.axis_index("cz")
    units, width = switching_coefficients.shape
    chunk = units // col_count
    tok_local = adjoint_vector.shape[0]
    tokens = tok_local * row_count

    cw = [(i, (i + 1) % cz_count) for i in range(cz_count)]
    ccw = [(i, (i - 1) % cz_count) for i in range(cz_count)]
    span = cy_count * chunk
    half_j = span // 2

    def piece(w, shift):
        return lax.dynamic_slice_in_dim(w, ((cz_here + shift) % cz_count) * span, span, axis=0)

    def reblock(weights):
        far = [piece(w, 2) for w in weights]
        n = len(weights)
        recv_cw = lax.ppermute([piece(w, 1) for w in weights] + [f[:half_j] for f in far], "cz", cw)
        recv_ccw = lax.ppermute([piece(w, 3) for w in weights] + [f[half_j:] for f in far], "cz", ccw)
        relay_cw = lax.ppermute(recv_cw[n:], "cz", cw)
        relay_ccw = lax.ppermute(recv_ccw[n:], "cz", ccw)
        return [
            (0, [piece(w, 0) for w in weights]),
            (-1, recv_cw[:n]),
            (1, recv_ccw[:n]),
            (2, [jnp.concatenate((a, b), axis=0) for a, b in zip(relay_cw, relay_ccw)]),
        ]

    gu_sources = reblock((switching_coefficients, expansion_coefficients))

    local_rows = pack_rows(
        trajectory_activations, kept_clusters_mask, piece_receiving_entry, piece_opening_position
    )
    xc = jnp.stack((local_rows, adjoint_vector))[None]
    xc_all = lax.all_gather(xc, ("row", "cz"), axis=0, tiled=True)
    xc_all = xc_all.reshape(row_count, cz_count, 2, tok_local, width)

    def xc_of(src):
        own = lax.dynamic_index_in_dim(xc_all, src % cz_count, 1, keepdims=False)
        return jnp.transpose(own, (1, 0, 2, 3)).reshape(2, tokens, width)

    dn = (((1,), (1,)), ((), ()))

    def width_sum(sources, which):
        out = [None] * len(which)
        for offset, pieces in sources:
            xc_src = xc_of(cz_here + offset)
            for m, use in enumerate(which):
                term = lax.dot_general(
                    pieces[m], xc_src[use], dn, preferred_element_type=jnp.float32
                )
                out[m] = term if out[m] is None else out[m] + term
        return [p.reshape(cy_count, chunk, tokens) for p in out]

    own_xc = xc_of(cz_here)
    x_panel = own_xc[0]
    cot_panel = own_xc[1]
    gu_parts = width_sum(gu_sources, (0, 0))
    wd_held, gu_parts = lax.optimization_barrier((contraction_coefficients, gu_parts))
    d_sources = reblock((wd_held,))

    cy_here = lax.axis_index("cy")
    up_ring = [(i, (i + 1) % cy_count) for i in range(cy_count)]
    down_ring = [(i, (i - 1) % cy_count) for i in range(cy_count)]
    half_t = tokens // 2

    split_t = (tokens // 2) // 128 * 128 + 128

    def ring_sum(parts):
        stacked = jnp.stack(parts, axis=1)

        def own_chunk(idx, lo, hi):
            return lax.dynamic_index_in_dim(stacked, idx % cy_count, 0, keepdims=False)[:, :, lo:hi]

        acc_up = own_chunk(cy_here - 1, 0, split_t)
        acc_down = own_chunk(cy_here + 1, split_t, tokens)
        for step in range(1, cy_count):
            got_up = lax.ppermute(acc_up, "cy", up_ring)
            got_down = lax.ppermute(acc_down, "cy", down_ring)
            acc_up = got_up + own_chunk(cy_here - step - 1, 0, split_t)
            acc_down = got_down + own_chunk(cy_here + step + 1, split_t, tokens)
        full = jnp.concatenate((acc_up, acc_down), axis=2)
        return [full[m] for m in range(len(parts))]

    gate_proj, up_proj = ring_sum(gu_parts)
    (grad_hidden,) = ring_sum(width_sum(d_sources, (1,)))
    sig_gate = jax.nn.sigmoid(gate_proj)
    hidden = (gate_proj * sig_gate * up_proj).astype(jnp.bfloat16)
    grad_gate = (grad_hidden * up_proj * sig_gate * (1.0 + gate_proj * (1.0 - sig_gate))).astype(
        jnp.bfloat16
    )
    grad_up = (grad_hidden * gate_proj * sig_gate).astype(jnp.bfloat16)
    acts = jnp.stack((hidden, grad_gate, grad_up))[None]
    acts_all = lax.all_gather(acts, ("cz", "cy"), axis=0, tiled=True)
    h_all, gg_all, gu_all = [acts_all[:, m].reshape(units, tokens) for m in range(3)]
    dn_f = (((0,), (0,)), ((), ()))
    mixed_part = lax.dot_general(h_all, contraction_coefficients, dn_f, preferred_element_type=jnp.float32)
    input_part = lax.dot_general(
        gg_all, switching_coefficients, dn_f, preferred_element_type=jnp.float32
    ) + lax.dot_general(gu_all, expansion_coefficients, dn_f, preferred_element_type=jnp.float32)
    dn_t = (((1,), (0,)), ((), ()))
    grad_w_down = lax.dot_general(h_all, cot_panel, dn_t, preferred_element_type=jnp.float32)
    grad_w_gate = lax.dot_general(gg_all, x_panel, dn_t, preferred_element_type=jnp.float32)
    grad_w_up = lax.dot_general(gu_all, x_panel, dn_t, preferred_element_type=jnp.float32)

    both = jnp.concatenate((mixed_part, input_part), axis=1)
    both = lax.psum_scatter(both, "row", scatter_dimension=0, tiled=True)
    mixed = (local_rows.astype(jnp.float32) + both[:, :width]).astype(jnp.bfloat16)
    grad_input = (adjoint_vector.astype(jnp.float32) + both[:, width:]).astype(jnp.bfloat16)
    return (
        mixed,
        grad_input,
        grad_w_gate,
        grad_w_up,
        grad_w_down,
    )


def solution(mesh):
    rows, cols = mesh.devices.shape
    mesh3 = Mesh(mesh.devices.reshape(rows, cols // CZ, CZ), ("row", "cy", "cz"))
    blk = P("row", ("cy", "cz"))
    return jax.shard_map(
        per_device,
        mesh=mesh3,
        in_specs=(blk, P(), P(), P(), blk, blk, blk, blk),
        out_specs=(blk, blk, blk, blk, blk),
        check_vma=False,
    )
```

```python
import jax
import jax.numpy as jnp
from jax import lax
from jax.sharding import Mesh
from jax.sharding import PartitionSpec as P

TOK_ROW = 80
BLOCK = 8
CLUSTER_PIECES = 5
CZ = 4


def piece_recipients(kept_clusters_mask, piece_receiving_entry):
    cluster_sequence = kept_clusters_mask.shape[0]
    survival_indicator = jnp.broadcast_to(
        kept_clusters_mask[:, None] == 1, (cluster_sequence, CLUSTER_PIECES)
    ).reshape(-1)
    return jnp.where(survival_indicator, piece_receiving_entry, -1)


def slot_ranking(live_dest):
    per_source = live_dest.shape[1]
    same_dest = (live_dest[:, :, None] == live_dest[:, None, :]) & (live_dest[:, None, :] >= 0)
    positions = jnp.arange(per_source, dtype=jnp.int32)
    earlier = positions[None, :] < positions[:, None]
    return jnp.sum((same_dest & earlier[None, :, :]).astype(jnp.int32), axis=2)


def pack_rows(trajectory_activations, kept_clusters_mask, piece_receiving_entry, piece_opening_position):
    row_count = lax.axis_size("row")
    row_here = lax.axis_index("row")
    feature_cols = trajectory_activations.shape[1]
    within = jnp.arange(BLOCK, dtype=jnp.int32)
    receiving_entries_total = piece_recipients(kept_clusters_mask, piece_receiving_entry)
    per_source = receiving_entries_total.shape[0] // row_count
    live_dest = receiving_entries_total.reshape(row_count, per_source)
    slot_rank = slot_ranking(live_dest)
    capacity = CLUSTER_PIECES * BLOCK
    my_dest = lax.dynamic_index_in_dim(live_dest, row_here, 0, keepdims=False)
    my_rank = lax.dynamic_index_in_dim(slot_rank, row_here, 0, keepdims=False)
    bucket_row = my_dest * capacity + my_rank * BLOCK
    bucket_row = jnp.where(
        my_dest[:, None] >= 0, bucket_row[:, None] + within[None, :], -1
    ).reshape(-1)
    selector = (
        jnp.arange(row_count * capacity, dtype=jnp.int32)[:, None] == bucket_row[None, :]
    ).astype(jnp.bfloat16)
    bucket = jnp.dot(selector, trajectory_activations, preferred_element_type=jnp.float32).astype(
        jnp.bfloat16
    )
    arrived = lax.all_to_all(
        bucket.reshape(row_count, capacity, feature_cols),
        "row",
        split_axis=0,
        concat_axis=0,
        tiled=True,
    )
    offsets = piece_opening_position.reshape(row_count, per_source)
    slot_ids = jnp.arange(CLUSTER_PIECES, dtype=jnp.int32)
    matched = (live_dest[:, None, :] == row_here) & (
        slot_rank[:, None, :] == slot_ids[None, :, None]
    )
    present = jnp.any(matched, axis=2)
    first_token = jnp.sum(jnp.where(matched, offsets[:, None, :], 0), axis=2)
    token_of = jnp.where(
        present[:, :, None], first_token[:, :, None] + within[None, None, :], -1
    ).reshape(-1)
    placing = (jnp.arange(TOK_ROW, dtype=jnp.int32)[:, None] == token_of[None, :]).astype(
        jnp.bfloat16
    )
    flat_arrived = arrived.reshape(row_count * capacity, feature_cols)
    return jnp.dot(placing, flat_arrived, preferred_element_type=jnp.float32).astype(jnp.bfloat16)


def per_device(
    trajectory_activations,
    kept_clusters_mask,
    piece_receiving_entry,
    piece_opening_position,
    switching_coefficients,
    expansion_coefficients,
    contraction_coefficients,
    adjoint_vector,
):
    row_count = lax.axis_size("row")
    cy_count = lax.axis_size("cy")
    cz_count = lax.axis_size("cz")
    col_count = cy_count * cz_count
    cz_here = lax.axis_index("cz")
    units, width = switching_coefficients.shape
    chunk = units // col_count
    tok_local = adjoint_vector.shape[0]
    tokens = tok_local * row_count

    cw = [(i, (i + 1) % cz_count) for i in range(cz_count)]
    ccw = [(i, (i - 1) % cz_count) for i in range(cz_count)]
    span = cy_count * chunk
    half_j = span // 2

    def piece(w, shift):
        return lax.dynamic_slice_in_dim(w, ((cz_here + shift) % cz_count) * span, span, axis=0)

    def reblock(weights):
        far = [piece(w, 2) for w in weights]
        n = len(weights)
        recv_cw = lax.ppermute([piece(w, 1) for w in weights] + [f[:half_j] for f in far], "cz", cw)
        recv_ccw = lax.ppermute([piece(w, 3) for w in weights] + [f[half_j:] for f in far], "cz", ccw)
        relay_cw = lax.ppermute(recv_cw[n:], "cz", cw)
        relay_ccw = lax.ppermute(recv_ccw[n:], "cz", ccw)
        return [
            (0, [piece(w, 0) for w in weights]),
            (-1, recv_cw[:n]),
            (1, recv_ccw[:n]),
            (2, [jnp.concatenate((a, b), axis=0) for a, b in zip(relay_cw, relay_ccw)]),
        ]

    gu_sources = reblock((switching_coefficients, expansion_coefficients))

    local_rows = pack_rows(
        trajectory_activations, kept_clusters_mask, piece_receiving_entry, piece_opening_position
    )
    xc = jnp.stack((local_rows, adjoint_vector))[None]
    xc_row = lax.all_gather(xc, "row", axis=0, tiled=True)
    xc_mine = jnp.transpose(xc_row, (1, 0, 2, 3)).reshape(2, tokens, width)
    xc_all = lax.all_gather(xc_mine[None], "cz", axis=0, tiled=True)

    def xc_of(src):
        if src is cz_here:
            return xc_mine
        return lax.dynamic_index_in_dim(xc_all, src % cz_count, 0, keepdims=False)

    dn = (((1,), (1,)), ((), ()))

    def width_sum(sources, which):
        out = [None] * len(which)
        for offset, pieces in sources:
            xc_src = xc_of(cz_here + offset) if offset else xc_mine
            for m, use in enumerate(which):
                term = lax.dot_general(
                    pieces[m], xc_src[use], dn, preferred_element_type=jnp.float32
                )
                out[m] = term if out[m] is None else out[m] + term
        return [p.reshape(cy_count, chunk, tokens) for p in out]

    own_xc = xc_mine
    x_panel = own_xc[0]
    cot_panel = own_xc[1]
    gu_parts = width_sum(gu_sources, (0, 0))
    wd_held, gu_parts = lax.optimization_barrier((contraction_coefficients, gu_parts))
    d_sources = reblock((wd_held,))

    cy_here = lax.axis_index("cy")
    up_ring = [(i, (i + 1) % cy_count) for i in range(cy_count)]
    down_ring = [(i, (i - 1) % cy_count) for i in range(cy_count)]
    half_t = tokens // 2

    def ring_sum(parts):
        def own_chunk(idx, lo, hi):
            return [lax.dynamic_index_in_dim(p, idx % cy_count, 0, keepdims=False)[:, lo:hi] for p in parts]

        acc_up = own_chunk(cy_here - 1, 0, half_t)
        acc_down = own_chunk(cy_here + 1, half_t, tokens)
        for step in range(1, cy_count):
            got_up = lax.ppermute(acc_up, "cy", up_ring)
            got_down = lax.ppermute(acc_down, "cy", down_ring)
            mine_up = own_chunk(cy_here - step - 1, 0, half_t)
            mine_down = own_chunk(cy_here + step + 1, half_t, tokens)
            acc_up = [a + b for a, b in zip(got_up, mine_up)]
            acc_down = [a + b for a, b in zip(got_down, mine_down)]
        return [jnp.concatenate((a, b), axis=1) for a, b in zip(acc_up, acc_down)]

    gate_proj, up_proj = ring_sum(gu_parts)
    (grad_hidden,) = ring_sum(width_sum(d_sources, (1,)))
    sig_gate = jax.nn.sigmoid(gate_proj)
    hidden = (gate_proj * sig_gate * up_proj).astype(jnp.bfloat16)
    grad_gate = (grad_hidden * up_proj * sig_gate * (1.0 + gate_proj * (1.0 - sig_gate))).astype(
        jnp.bfloat16
    )
    grad_up = (grad_hidden * gate_proj * sig_gate).astype(jnp.bfloat16)
    acts = jnp.stack((hidden, grad_gate, grad_up))[None]
    acts_all = lax.all_gather(acts, ("cz", "cy"), axis=0, tiled=True)
    h_all, gg_all, gu_all = [acts_all[:, m].reshape(units, tokens) for m in range(3)]
    dn_f = (((0,), (0,)), ((), ()))
    mixed_part = lax.dot_general(h_all, contraction_coefficients, dn_f, preferred_element_type=jnp.float32)
    input_part = lax.dot_general(
        gg_all, switching_coefficients, dn_f, preferred_element_type=jnp.float32
    ) + lax.dot_general(gu_all, expansion_coefficients, dn_f, preferred_element_type=jnp.float32)
    dn_t = (((1,), (0,)), ((), ()))
    grad_w_down = lax.dot_general(h_all, cot_panel, dn_t, preferred_element_type=jnp.float32)
    grad_w_gate = lax.dot_general(gg_all, x_panel, dn_t, preferred_element_type=jnp.float32)
    grad_w_up = lax.dot_general(gu_all, x_panel, dn_t, preferred_element_type=jnp.float32)

    both = jnp.concatenate((mixed_part, input_part), axis=1)
    both = lax.psum_scatter(both, "row", scatter_dimension=0, tiled=True)
    mixed = (local_rows.astype(jnp.float32) + both[:, :width]).astype(jnp.bfloat16)
    grad_input = (adjoint_vector.astype(jnp.float32) + both[:, width:]).astype(jnp.bfloat16)
    return (
        mixed,
        grad_input,
        grad_w_gate,
        grad_w_up,
        grad_w_down,
    )


def solution(mesh):
    rows, cols = mesh.devices.shape
    mesh3 = Mesh(mesh.devices.reshape(rows, cols // CZ, CZ), ("row", "cy", "cz"))
    blk = P("row", ("cy", "cz"))
    return jax.shard_map(
        per_device,
        mesh=mesh3,
        in_specs=(blk, P(), P(), P(), blk, blk, blk, blk),
        out_specs=(blk, blk, blk, blk, blk),
        check_vma=False,
    )
```

```python
import jax
import jax.numpy as jnp
from jax import lax
from jax.sharding import Mesh
from jax.sharding import PartitionSpec as P

TOK_ROW = 80
BLOCK = 8
CLUSTER_PIECES = 5
CZ = 4


def piece_recipients(kept_clusters_mask, piece_receiving_entry):
    cluster_sequence = kept_clusters_mask.shape[0]
    survival_indicator = jnp.broadcast_to(
        kept_clusters_mask[:, None] == 1, (cluster_sequence, CLUSTER_PIECES)
    ).reshape(-1)
    return jnp.where(survival_indicator, piece_receiving_entry, -1)


def slot_ranking(live_dest):
    per_source = live_dest.shape[1]
    same_dest = (live_dest[:, :, None] == live_dest[:, None, :]) & (live_dest[:, None, :] >= 0)
    positions = jnp.arange(per_source, dtype=jnp.int32)
    earlier = positions[None, :] < positions[:, None]
    return jnp.sum((same_dest & earlier[None, :, :]).astype(jnp.int32), axis=2)


def pack_rows(trajectory_activations, kept_clusters_mask, piece_receiving_entry, piece_opening_position):
    row_count = lax.axis_size("row")
    row_here = lax.axis_index("row")
    feature_cols = trajectory_activations.shape[1]
    within = jnp.arange(BLOCK, dtype=jnp.int32)
    receiving_entries_total = piece_recipients(kept_clusters_mask, piece_receiving_entry)
    per_source = receiving_entries_total.shape[0] // row_count
    live_dest = receiving_entries_total.reshape(row_count, per_source)
    slot_rank = slot_ranking(live_dest)
    capacity = CLUSTER_PIECES * BLOCK
    my_dest = lax.dynamic_index_in_dim(live_dest, row_here, 0, keepdims=False)
    my_rank = lax.dynamic_index_in_dim(slot_rank, row_here, 0, keepdims=False)
    bucket_row = my_dest * capacity + my_rank * BLOCK
    bucket_row = jnp.where(
        my_dest[:, None] >= 0, bucket_row[:, None] + within[None, :], -1
    ).reshape(-1)
    selector = (
        jnp.arange(row_count * capacity, dtype=jnp.int32)[:, None] == bucket_row[None, :]
    ).astype(jnp.bfloat16)
    bucket = jnp.dot(selector, trajectory_activations, preferred_element_type=jnp.float32).astype(
        jnp.bfloat16
    )
    arrived = lax.all_to_all(
        bucket.reshape(row_count, capacity, feature_cols),
        "row",
        split_axis=0,
        concat_axis=0,
        tiled=True,
    )
    offsets = piece_opening_position.reshape(row_count, per_source)
    slot_ids = jnp.arange(CLUSTER_PIECES, dtype=jnp.int32)
    matched = (live_dest[:, None, :] == row_here) & (
        slot_rank[:, None, :] == slot_ids[None, :, None]
    )
    present = jnp.any(matched, axis=2)
    first_token = jnp.sum(jnp.where(matched, offsets[:, None, :], 0), axis=2)
    token_of = jnp.where(
        present[:, :, None], first_token[:, :, None] + within[None, None, :], -1
    ).reshape(-1)
    placing = (jnp.arange(TOK_ROW, dtype=jnp.int32)[:, None] == token_of[None, :]).astype(
        jnp.bfloat16
    )
    flat_arrived = arrived.reshape(row_count * capacity, feature_cols)
    return jnp.dot(placing, flat_arrived, preferred_element_type=jnp.float32).astype(jnp.bfloat16)


def ring_gather(x, axis):
    n = lax.axis_size(axis)
    here = lax.axis_index(axis)
    right = [(i, (i + 1) % n) for i in range(n)]
    left = [(i, (i - 1) % n) for i in range(n)]
    from_left = lax.ppermute(x, axis, right)
    from_right = lax.ppermute(x, axis, left)
    from_far = lax.ppermute(from_left, axis, right)
    out = jnp.zeros((n,) + x.shape, x.dtype)
    for shift, part in ((0, x), (-1, from_left), (1, from_right), (2, from_far)):
        out = lax.dynamic_update_index_in_dim(out, part, (here + shift) % n, 0)
    return out


def per_device(
    trajectory_activations,
    kept_clusters_mask,
    piece_receiving_entry,
    piece_opening_position,
    switching_coefficients,
    expansion_coefficients,
    contraction_coefficients,
    adjoint_vector,
):
    row_count = lax.axis_size("row")
    cy_count = lax.axis_size("cy")
    cz_count = lax.axis_size("cz")
    col_count = cy_count * cz_count
    cz_here = lax.axis_index("cz")
    units, width = switching_coefficients.shape
    chunk = units // col_count
    tok_local = adjoint_vector.shape[0]
    tokens = tok_local * row_count

    cw = [(i, (i + 1) % cz_count) for i in range(cz_count)]
    ccw = [(i, (i - 1) % cz_count) for i in range(cz_count)]
    span = cy_count * chunk
    half_j = span // 2

    def piece(w, shift):
        return lax.dynamic_slice_in_dim(w, ((cz_here + shift) % cz_count) * span, span, axis=0)

    def reblock(weights):
        far = [piece(w, 2) for w in weights]
        n = len(weights)
        recv_cw = lax.ppermute([piece(w, 1) for w in weights] + [f[:half_j] for f in far], "cz", cw)
        recv_ccw = lax.ppermute([piece(w, 3) for w in weights] + [f[half_j:] for f in far], "cz", ccw)
        relay_cw = lax.ppermute(recv_cw[n:], "cz", cw)
        relay_ccw = lax.ppermute(recv_ccw[n:], "cz", ccw)
        return [
            (0, [piece(w, 0) for w in weights]),
            (-1, recv_cw[:n]),
            (1, recv_ccw[:n]),
            (2, [jnp.concatenate((a, b), axis=0) for a, b in zip(relay_cw, relay_ccw)]),
        ]

    gu_sources = reblock((switching_coefficients, expansion_coefficients))

    local_rows = pack_rows(
        trajectory_activations, kept_clusters_mask, piece_receiving_entry, piece_opening_position
    )
    xc = jnp.stack((local_rows, adjoint_vector))[None]
    xc_all = lax.all_gather(xc, ("row", "cz"), axis=0, tiled=True)
    xc_all = xc_all.reshape(row_count, cz_count, 2, tok_local, width)

    def xc_of(src):
        own = lax.dynamic_index_in_dim(xc_all, src % cz_count, 1, keepdims=False)
        return jnp.transpose(own, (1, 0, 2, 3)).reshape(2, tokens, width)

    dn = (((1,), (1,)), ((), ()))

    def width_sum(sources, which):
        out = [None] * len(which)
        for offset, pieces in sources:
            xc_src = xc_of(cz_here + offset)
            for m, use in enumerate(which):
                term = lax.dot_general(
                    pieces[m], xc_src[use], dn, preferred_element_type=jnp.float32
                )
                out[m] = term if out[m] is None else out[m] + term
        return [p.reshape(cy_count, chunk, tokens) for p in out]

    own_xc = xc_of(cz_here)
    x_panel = own_xc[0]
    cot_panel = own_xc[1]
    gu_parts = width_sum(gu_sources, (0, 0))
    wd_held, gu_parts = lax.optimization_barrier((contraction_coefficients, gu_parts))
    d_sources = reblock((wd_held,))

    cy_here = lax.axis_index("cy")
    up_ring = [(i, (i + 1) % cy_count) for i in range(cy_count)]
    down_ring = [(i, (i - 1) % cy_count) for i in range(cy_count)]
    half_t = tokens // 2

    def ring_sum(parts):
        def own_chunk(idx, lo, hi):
            return [lax.dynamic_index_in_dim(p, idx % cy_count, 0, keepdims=False)[:, lo:hi] for p in parts]

        acc_up = own_chunk(cy_here - 1, 0, half_t)
        acc_down = own_chunk(cy_here + 1, half_t, tokens)
        for step in range(1, cy_count):
            got_up = lax.ppermute(acc_up, "cy", up_ring)
            got_down = lax.ppermute(acc_down, "cy", down_ring)
            mine_up = own_chunk(cy_here - step - 1, 0, half_t)
            mine_down = own_chunk(cy_here + step + 1, half_t, tokens)
            acc_up = [a + b for a, b in zip(got_up, mine_up)]
            acc_down = [a + b for a, b in zip(got_down, mine_down)]
        return [jnp.concatenate((a, b), axis=1) for a, b in zip(acc_up, acc_down)]

    gate_proj, up_proj = ring_sum(gu_parts)
    (grad_hidden,) = ring_sum(width_sum(d_sources, (1,)))
    sig_gate = jax.nn.sigmoid(gate_proj)
    hidden = (gate_proj * sig_gate * up_proj).astype(jnp.bfloat16)
    grad_gate = (grad_hidden * up_proj * sig_gate * (1.0 + gate_proj * (1.0 - sig_gate))).astype(
        jnp.bfloat16
    )
    grad_up = (grad_hidden * gate_proj * sig_gate).astype(jnp.bfloat16)
    grads = jnp.stack((grad_gate, grad_up))[None]
    grads_all = lax.all_gather(grads, ("cz", "cy"), axis=0, tiled=True)
    gg_all, gu_all = [grads_all[:, m].reshape(units, tokens) for m in range(2)]
    h_all = ring_gather(ring_gather(hidden, "cy"), "cz").reshape(units, tokens)
    dn_f = (((0,), (0,)), ((), ()))
    mixed_part = lax.dot_general(h_all, contraction_coefficients, dn_f, preferred_element_type=jnp.float32)
    input_part = lax.dot_general(
        gg_all, switching_coefficients, dn_f, preferred_element_type=jnp.float32
    ) + lax.dot_general(gu_all, expansion_coefficients, dn_f, preferred_element_type=jnp.float32)
    dn_t = (((1,), (0,)), ((), ()))
    grad_w_down = lax.dot_general(h_all, cot_panel, dn_t, preferred_element_type=jnp.float32)
    grad_w_gate = lax.dot_general(gg_all, x_panel, dn_t, preferred_element_type=jnp.float32)
    grad_w_up = lax.dot_general(gu_all, x_panel, dn_t, preferred_element_type=jnp.float32)

    both = jnp.concatenate((mixed_part, input_part), axis=1)
    both = lax.psum_scatter(both, "row", scatter_dimension=0, tiled=True)
    mixed = (local_rows.astype(jnp.float32) + both[:, :width]).astype(jnp.bfloat16)
    grad_input = (adjoint_vector.astype(jnp.float32) + both[:, width:]).astype(jnp.bfloat16)
    return (
        mixed,
        grad_input,
        grad_w_gate,
        grad_w_up,
        grad_w_down,
    )


def solution(mesh):
    rows, cols = mesh.devices.shape
    mesh3 = Mesh(mesh.devices.reshape(rows, cols // CZ, CZ), ("row", "cy", "cz"))
    blk = P("row", ("cy", "cz"))
    return jax.shard_map(
        per_device,
        mesh=mesh3,
        in_specs=(blk, P(), P(), P(), blk, blk, blk, blk),
        out_specs=(blk, blk, blk, blk, blk),
        check_vma=False,
    )
```

```python
import jax
import jax.numpy as jnp
from jax import lax
from jax.sharding import Mesh
from jax.sharding import PartitionSpec as P

TOK_ROW = 80
BLOCK = 8
CLUSTER_PIECES = 5
CZ = 4


def piece_recipients(kept_clusters_mask, piece_receiving_entry):
    cluster_sequence = kept_clusters_mask.shape[0]
    survival_indicator = jnp.broadcast_to(
        kept_clusters_mask[:, None] == 1, (cluster_sequence, CLUSTER_PIECES)
    ).reshape(-1)
    return jnp.where(survival_indicator, piece_receiving_entry, -1)


def slot_ranking(live_dest):
    per_source = live_dest.shape[1]
    same_dest = (live_dest[:, :, None] == live_dest[:, None, :]) & (live_dest[:, None, :] >= 0)
    positions = jnp.arange(per_source, dtype=jnp.int32)
    earlier = positions[None, :] < positions[:, None]
    return jnp.sum((same_dest & earlier[None, :, :]).astype(jnp.int32), axis=2)


def pack_rows(trajectory_activations, kept_clusters_mask, piece_receiving_entry, piece_opening_position):
    row_count = lax.axis_size("row")
    row_here = lax.axis_index("row")
    feature_cols = trajectory_activations.shape[1]
    within = jnp.arange(BLOCK, dtype=jnp.int32)
    receiving_entries_total = piece_recipients(kept_clusters_mask, piece_receiving_entry)
    per_source = receiving_entries_total.shape[0] // row_count
    live_dest = receiving_entries_total.reshape(row_count, per_source)
    slot_rank = slot_ranking(live_dest)
    capacity = CLUSTER_PIECES * BLOCK
    my_dest = lax.dynamic_index_in_dim(live_dest, row_here, 0, keepdims=False)
    my_rank = lax.dynamic_index_in_dim(slot_rank, row_here, 0, keepdims=False)
    bucket_row = my_dest * capacity + my_rank * BLOCK
    bucket_row = jnp.where(
        my_dest[:, None] >= 0, bucket_row[:, None] + within[None, :], -1
    ).reshape(-1)
    selector = (
        jnp.arange(row_count * capacity, dtype=jnp.int32)[:, None] == bucket_row[None, :]
    ).astype(jnp.bfloat16)
    bucket = jnp.dot(selector, trajectory_activations, preferred_element_type=jnp.float32).astype(
        jnp.bfloat16
    )
    arrived = lax.all_to_all(
        bucket.reshape(row_count, capacity, feature_cols),
        "row",
        split_axis=0,
        concat_axis=0,
        tiled=True,
    )
    offsets = piece_opening_position.reshape(row_count, per_source)
    slot_ids = jnp.arange(CLUSTER_PIECES, dtype=jnp.int32)
    matched = (live_dest[:, None, :] == row_here) & (
        slot_rank[:, None, :] == slot_ids[None, :, None]
    )
    present = jnp.any(matched, axis=2)
    first_token = jnp.sum(jnp.where(matched, offsets[:, None, :], 0), axis=2)
    token_of = jnp.where(
        present[:, :, None], first_token[:, :, None] + within[None, None, :], -1
    ).reshape(-1)
    placing = (jnp.arange(TOK_ROW, dtype=jnp.int32)[:, None] == token_of[None, :]).astype(
        jnp.bfloat16
    )
    flat_arrived = arrived.reshape(row_count * capacity, feature_cols)
    return jnp.dot(placing, flat_arrived, preferred_element_type=jnp.float32).astype(jnp.bfloat16)


def per_device(
    trajectory_activations,
    kept_clusters_mask,
    piece_receiving_entry,
    piece_opening_position,
    switching_coefficients,
    expansion_coefficients,
    contraction_coefficients,
    adjoint_vector,
):
    row_count = lax.axis_size("row")
    cy_count = lax.axis_size("cy")
    cz_count = lax.axis_size("cz")
    col_count = cy_count * cz_count
    cz_here = lax.axis_index("cz")
    units, width = switching_coefficients.shape
    chunk = units // col_count
    tok_local = adjoint_vector.shape[0]
    tokens = tok_local * row_count

    cw = [(i, (i + 1) % cz_count) for i in range(cz_count)]
    ccw = [(i, (i - 1) % cz_count) for i in range(cz_count)]
    span = cy_count * chunk
    half_j = span // 2

    def piece(w, shift):
        return lax.dynamic_slice_in_dim(w, ((cz_here + shift) % cz_count) * span, span, axis=0)

    def reblock(weights):
        far = [piece(w, 2) for w in weights]
        n = len(weights)
        recv_cw = lax.ppermute([piece(w, 1) for w in weights] + [f[:half_j] for f in far], "cz", cw)
        recv_ccw = lax.ppermute([piece(w, 3) for w in weights] + [f[half_j:] for f in far], "cz", ccw)
        relay_cw = lax.ppermute(recv_cw[n:], "cz", cw)
        relay_ccw = lax.ppermute(recv_ccw[n:], "cz", ccw)
        return [
            (0, [piece(w, 0) for w in weights]),
            (-1, recv_cw[:n]),
            (1, recv_ccw[:n]),
            (2, [jnp.concatenate((a, b), axis=0) for a, b in zip(relay_cw, relay_ccw)]),
        ]

    gu_sources = reblock((switching_coefficients, expansion_coefficients))

    blocks = piece_receiving_entry.shape[0]
    kept = kept_clusters_mask[jnp.arange(blocks, dtype=jnp.int32) // CLUSTER_PIECES] == 1
    first = piece_receiving_entry * TOK_ROW + piece_opening_position
    within = jnp.arange(BLOCK, dtype=jnp.int32)
    target = jnp.where(kept[:, None], first[:, None] + within[None, :], -1).reshape(-1)
    select = (jnp.arange(tokens, dtype=jnp.int32)[:, None] == target[None, :]).astype(jnp.bfloat16)
    roll_local = trajectory_activations.shape[0]
    ta = jnp.concatenate((trajectory_activations, adjoint_vector), axis=0)[None]
    ta_all = lax.all_gather(ta, ("row", "cz"), axis=0, tiled=True)
    ta_all = ta_all.reshape(row_count, cz_count, roll_local + tok_local, width)

    def xc_of(src):
        blk = lax.dynamic_index_in_dim(ta_all, src % cz_count, 1, keepdims=False)
        roll = blk[:, :roll_local].reshape(row_count * roll_local, width)
        packed = jnp.dot(select, roll, preferred_element_type=jnp.float32).astype(jnp.bfloat16)
        return jnp.stack((packed, blk[:, roll_local:].reshape(tokens, width)))

    dn = (((1,), (1,)), ((), ()))

    def width_sum(sources, which):
        out = [None] * len(which)
        for offset, pieces in sources:
            xc_src = xc_of(cz_here + offset)
            for m, use in enumerate(which):
                term = lax.dot_general(
                    pieces[m], xc_src[use], dn, preferred_element_type=jnp.float32
                )
                out[m] = term if out[m] is None else out[m] + term
        return [p.reshape(cy_count, chunk, tokens) for p in out]

    own_xc = xc_of(cz_here)
    x_panel = own_xc[0]
    cot_panel = own_xc[1]
    local_rows = lax.dynamic_slice_in_dim(x_panel, lax.axis_index("row") * tok_local, tok_local, axis=0)
    gu_parts = width_sum(gu_sources, (0, 0))
    wd_held, gu_parts = lax.optimization_barrier((contraction_coefficients, gu_parts))
    d_sources = reblock((wd_held,))

    cy_here = lax.axis_index("cy")
    up_ring = [(i, (i + 1) % cy_count) for i in range(cy_count)]
    down_ring = [(i, (i - 1) % cy_count) for i in range(cy_count)]
    half_t = tokens // 2

    def ring_sum(parts):
        def own_chunk(idx, lo, hi):
            return [lax.dynamic_index_in_dim(p, idx % cy_count, 0, keepdims=False)[:, lo:hi] for p in parts]

        acc_up = own_chunk(cy_here - 1, 0, half_t)
        acc_down = own_chunk(cy_here + 1, half_t, tokens)
        for step in range(1, cy_count):
            got_up = lax.ppermute(acc_up, "cy", up_ring)
            got_down = lax.ppermute(acc_down, "cy", down_ring)
            mine_up = own_chunk(cy_here - step - 1, 0, half_t)
            mine_down = own_chunk(cy_here + step + 1, half_t, tokens)
            acc_up = [a + b for a, b in zip(got_up, mine_up)]
            acc_down = [a + b for a, b in zip(got_down, mine_down)]
        return [jnp.concatenate((a, b), axis=1) for a, b in zip(acc_up, acc_down)]

    gate_proj, up_proj = ring_sum(gu_parts)
    (grad_hidden,) = ring_sum(width_sum(d_sources, (1,)))
    sig_gate = jax.nn.sigmoid(gate_proj)
    hidden = (gate_proj * sig_gate * up_proj).astype(jnp.bfloat16)
    grad_gate = (grad_hidden * up_proj * sig_gate * (1.0 + gate_proj * (1.0 - sig_gate))).astype(
        jnp.bfloat16
    )
    grad_up = (grad_hidden * gate_proj * sig_gate).astype(jnp.bfloat16)
    acts = jnp.stack((hidden, grad_gate, grad_up))[None]
    acts_all = lax.all_gather(acts, ("cz", "cy"), axis=0, tiled=True)
    h_all, gg_all, gu_all = [acts_all[:, m].reshape(units, tokens) for m in range(3)]
    dn_f = (((0,), (0,)), ((), ()))
    mixed_part = lax.dot_general(h_all, contraction_coefficients, dn_f, preferred_element_type=jnp.float32)
    input_part = lax.dot_general(
        gg_all, switching_coefficients, dn_f, preferred_element_type=jnp.float32
    ) + lax.dot_general(gu_all, expansion_coefficients, dn_f, preferred_element_type=jnp.float32)
    dn_t = (((1,), (0,)), ((), ()))
    grad_w_down = lax.dot_general(h_all, cot_panel, dn_t, preferred_element_type=jnp.float32)
    grad_w_gate = lax.dot_general(gg_all, x_panel, dn_t, preferred_element_type=jnp.float32)
    grad_w_up = lax.dot_general(gu_all, x_panel, dn_t, preferred_element_type=jnp.float32)

    both = jnp.concatenate((mixed_part, input_part), axis=1)
    both = lax.psum_scatter(both, "row", scatter_dimension=0, tiled=True)
    mixed = (local_rows.astype(jnp.float32) + both[:, :width]).astype(jnp.bfloat16)
    grad_input = (adjoint_vector.astype(jnp.float32) + both[:, width:]).astype(jnp.bfloat16)
    return (
        mixed,
        grad_input,
        grad_w_gate,
        grad_w_up,
        grad_w_down,
    )


def solution(mesh):
    rows, cols = mesh.devices.shape
    mesh3 = Mesh(mesh.devices.reshape(rows, cols // CZ, CZ), ("row", "cy", "cz"))
    blk = P("row", ("cy", "cz"))
    return jax.shard_map(
        per_device,
        mesh=mesh3,
        in_specs=(blk, P(), P(), P(), blk, blk, blk, blk),
        out_specs=(blk, blk, blk, blk, blk),
        check_vma=False,
    )
```

```python
import jax
import jax.numpy as jnp
from jax import lax
from jax.sharding import Mesh
from jax.sharding import PartitionSpec as P

TOK_ROW = 80
BLOCK = 8
CLUSTER_PIECES = 5
CZ = 4


def piece_recipients(kept_clusters_mask, piece_receiving_entry):
    cluster_sequence = kept_clusters_mask.shape[0]
    survival_indicator = jnp.broadcast_to(
        kept_clusters_mask[:, None] == 1, (cluster_sequence, CLUSTER_PIECES)
    ).reshape(-1)
    return jnp.where(survival_indicator, piece_receiving_entry, -1)


def slot_ranking(live_dest):
    per_source = live_dest.shape[1]
    same_dest = (live_dest[:, :, None] == live_dest[:, None, :]) & (live_dest[:, None, :] >= 0)
    positions = jnp.arange(per_source, dtype=jnp.int32)
    earlier = positions[None, :] < positions[:, None]
    return jnp.sum((same_dest & earlier[None, :, :]).astype(jnp.int32), axis=2)


def pack_rows(trajectory_activations, kept_clusters_mask, piece_receiving_entry, piece_opening_position):
    row_count = lax.axis_size("row")
    row_here = lax.axis_index("row")
    feature_cols = trajectory_activations.shape[1]
    within = jnp.arange(BLOCK, dtype=jnp.int32)
    receiving_entries_total = piece_recipients(kept_clusters_mask, piece_receiving_entry)
    per_source = receiving_entries_total.shape[0] // row_count
    live_dest = receiving_entries_total.reshape(row_count, per_source)
    slot_rank = slot_ranking(live_dest)
    capacity = CLUSTER_PIECES * BLOCK
    my_dest = lax.dynamic_index_in_dim(live_dest, row_here, 0, keepdims=False)
    my_rank = lax.dynamic_index_in_dim(slot_rank, row_here, 0, keepdims=False)
    bucket_row = my_dest * capacity + my_rank * BLOCK
    bucket_row = jnp.where(
        my_dest[:, None] >= 0, bucket_row[:, None] + within[None, :], -1
    ).reshape(-1)
    selector = (
        jnp.arange(row_count * capacity, dtype=jnp.int32)[:, None] == bucket_row[None, :]
    ).astype(jnp.bfloat16)
    bucket = jnp.dot(selector, trajectory_activations, preferred_element_type=jnp.float32).astype(
        jnp.bfloat16
    )
    arrived = lax.all_to_all(
        bucket.reshape(row_count, capacity, feature_cols),
        "row",
        split_axis=0,
        concat_axis=0,
        tiled=True,
    )
    offsets = piece_opening_position.reshape(row_count, per_source)
    slot_ids = jnp.arange(CLUSTER_PIECES, dtype=jnp.int32)
    matched = (live_dest[:, None, :] == row_here) & (
        slot_rank[:, None, :] == slot_ids[None, :, None]
    )
    present = jnp.any(matched, axis=2)
    first_token = jnp.sum(jnp.where(matched, offsets[:, None, :], 0), axis=2)
    token_of = jnp.where(
        present[:, :, None], first_token[:, :, None] + within[None, None, :], -1
    ).reshape(-1)
    placing = (jnp.arange(TOK_ROW, dtype=jnp.int32)[:, None] == token_of[None, :]).astype(
        jnp.bfloat16
    )
    flat_arrived = arrived.reshape(row_count * capacity, feature_cols)
    return jnp.dot(placing, flat_arrived, preferred_element_type=jnp.float32).astype(jnp.bfloat16)


def per_device(
    trajectory_activations,
    kept_clusters_mask,
    piece_receiving_entry,
    piece_opening_position,
    switching_coefficients,
    expansion_coefficients,
    contraction_coefficients,
    adjoint_vector,
):
    row_count = lax.axis_size("row")
    cy_count = lax.axis_size("cy")
    cz_count = lax.axis_size("cz")
    col_count = cy_count * cz_count
    cz_here = lax.axis_index("cz")
    units, width = switching_coefficients.shape
    chunk = units // col_count
    tok_local = adjoint_vector.shape[0]
    tokens = tok_local * row_count

    cw = [(i, (i + 1) % cz_count) for i in range(cz_count)]
    ccw = [(i, (i - 1) % cz_count) for i in range(cz_count)]
    span = cy_count * chunk
    half_j = span // 2

    def piece(w, shift):
        return lax.dynamic_slice_in_dim(w, ((cz_here + shift) % cz_count) * span, span, axis=0)

    def reblock(weights):
        far = [piece(w, 2) for w in weights]
        n = len(weights)
        recv_cw = lax.ppermute([piece(w, 1) for w in weights] + [f[:half_j] for f in far], "cz", cw)
        recv_ccw = lax.ppermute([piece(w, 3) for w in weights] + [f[half_j:] for f in far], "cz", ccw)
        relay_cw = lax.ppermute(recv_cw[n:], "cz", cw)
        relay_ccw = lax.ppermute(recv_ccw[n:], "cz", ccw)
        return [
            (0, [piece(w, 0) for w in weights]),
            (-1, recv_cw[:n]),
            (1, recv_ccw[:n]),
            (2, [jnp.concatenate((a, b), axis=0) for a, b in zip(relay_cw, relay_ccw)]),
        ]

    gu_sources = reblock((switching_coefficients, expansion_coefficients))

    local_rows = pack_rows(
        trajectory_activations, kept_clusters_mask, piece_receiving_entry, piece_opening_position
    )
    xc = jnp.stack((local_rows, adjoint_vector))[None]
    xc_all = lax.all_gather(xc, ("cz", "row"), axis=0, tiled=True)
    xc_all = xc_all.reshape(cz_count, row_count, 2, tok_local, width)

    def xc_of(src):
        own = lax.dynamic_index_in_dim(xc_all, src % cz_count, 0, keepdims=False)
        return jnp.transpose(own, (1, 0, 2, 3)).reshape(2, tokens, width)

    dn = (((1,), (1,)), ((), ()))

    def width_sum(sources, which):
        out = [None] * len(which)
        for offset, pieces in sources:
            xc_src = xc_of(cz_here + offset)
            for m, use in enumerate(which):
                term = lax.dot_general(
                    pieces[m], xc_src[use], dn, preferred_element_type=jnp.float32
                )
                out[m] = term if out[m] is None else out[m] + term
        return [p.reshape(cy_count, chunk, tokens) for p in out]

    own_xc = xc_of(cz_here)
    x_panel = own_xc[0]
    cot_panel = own_xc[1]
    gu_parts = width_sum(gu_sources, (0, 0))
    wd_held, gu_parts = lax.optimization_barrier((contraction_coefficients, gu_parts))
    d_sources = reblock((wd_held,))

    cy_here = lax.axis_index("cy")
    up_ring = [(i, (i + 1) % cy_count) for i in range(cy_count)]
    down_ring = [(i, (i - 1) % cy_count) for i in range(cy_count)]
    half_t = tokens // 2

    def ring_sum(parts):
        def own_chunk(idx, lo, hi):
            return [lax.dynamic_index_in_dim(p, idx % cy_count, 0, keepdims=False)[:, lo:hi] for p in parts]

        acc_up = own_chunk(cy_here - 1, 0, half_t)
        acc_down = own_chunk(cy_here + 1, half_t, tokens)
        for step in range(1, cy_count):
            got_up = lax.ppermute(acc_up, "cy", up_ring)
            got_down = lax.ppermute(acc_down, "cy", down_ring)
            mine_up = own_chunk(cy_here - step - 1, 0, half_t)
            mine_down = own_chunk(cy_here + step + 1, half_t, tokens)
            acc_up = [a + b for a, b in zip(got_up, mine_up)]
            acc_down = [a + b for a, b in zip(got_down, mine_down)]
        return [jnp.concatenate((a, b), axis=1) for a, b in zip(acc_up, acc_down)]

    gate_proj, up_proj = ring_sum(gu_parts)
    (grad_hidden,) = ring_sum(width_sum(d_sources, (1,)))
    sig_gate = jax.nn.sigmoid(gate_proj)
    hidden = (gate_proj * sig_gate * up_proj).astype(jnp.bfloat16)
    grad_gate = (grad_hidden * up_proj * sig_gate * (1.0 + gate_proj * (1.0 - sig_gate))).astype(
        jnp.bfloat16
    )
    grad_up = (grad_hidden * gate_proj * sig_gate).astype(jnp.bfloat16)
    acts = jnp.stack((hidden, grad_gate, grad_up))[None]
    acts_all = lax.all_gather(acts, ("cz", "cy"), axis=0, tiled=True)
    h_all, gg_all, gu_all = [acts_all[:, m].reshape(units, tokens) for m in range(3)]
    dn_f = (((0,), (0,)), ((), ()))
    mixed_part = lax.dot_general(h_all, contraction_coefficients, dn_f, preferred_element_type=jnp.float32)
    input_part = lax.dot_general(
        gg_all, switching_coefficients, dn_f, preferred_element_type=jnp.float32
    ) + lax.dot_general(gu_all, expansion_coefficients, dn_f, preferred_element_type=jnp.float32)
    dn_t = (((1,), (0,)), ((), ()))
    grad_w_down = lax.dot_general(h_all, cot_panel, dn_t, preferred_element_type=jnp.float32)
    grad_w_gate = lax.dot_general(gg_all, x_panel, dn_t, preferred_element_type=jnp.float32)
    grad_w_up = lax.dot_general(gu_all, x_panel, dn_t, preferred_element_type=jnp.float32)

    both = jnp.concatenate((mixed_part, input_part), axis=1)
    both = lax.psum_scatter(both, "row", scatter_dimension=0, tiled=True)
    mixed = (local_rows.astype(jnp.float32) + both[:, :width]).astype(jnp.bfloat16)
    grad_input = (adjoint_vector.astype(jnp.float32) + both[:, width:]).astype(jnp.bfloat16)
    return (
        mixed,
        grad_input,
        grad_w_gate,
        grad_w_up,
        grad_w_down,
    )


def solution(mesh):
    rows, cols = mesh.devices.shape
    mesh3 = Mesh(mesh.devices.reshape(rows, cols // CZ, CZ), ("row", "cy", "cz"))
    blk = P("row", ("cy", "cz"))
    return jax.shard_map(
        per_device,
        mesh=mesh3,
        in_specs=(blk, P(), P(), P(), blk, blk, blk, blk),
        out_specs=(blk, blk, blk, blk, blk),
        check_vma=False,
    )
```
